512 devices in a mesh: tile: 128 (over z, y, core), band: 4 (over x).
Axes of the slice: x: 4, y: 4, z: 16, core: 2. Of those that a mesh axis runs over, the one named last changes fastest.
Arguments:
- sky_model: bfloat16 [4, 262144, 128], P('band', 'tile'), may hold values from -6 to 6
- observed: bfloat16 [4, 128, 1024, 128], P('band', 'tile'), may hold values from -6 to 6
- row_weight: float32 [4, 128, 128], P('band', 'tile'), may hold values from 0.1 to 1
- foot_owner: int32 [4, 128, 1024, 1], P('band', 'tile'), may hold values from 0 to 127; in each aligned block of 1024 rows (0 to 1023, 1024 to 2047, ..., all dimensions but the last counted through in order) at most 16 rows name the same one
- foot_local: int32 [4, 128, 1024], P('band', 'tile'), may hold values from 0 to 2047
- row_offset: int32 [4, 128], P('band', 'tile'), may hold values from -4 to 4
- exposure_of: int32 [4, 128], P('band', 'tile'), may hold values from 0 to 255
- amplitude: float32 [4, 256], replicated, may hold values from 0.25 to 1
- subpixel_shift: float32 [256], replicated, may hold values from 0.05 to 0.95
- column_profile: float32 [256, 4, 25], replicated, may hold values from 0.05 to 0.3
- row_profile: float32 [256, 4, 25], replicated, may hold values from 0.05 to 0.3
Outputs:
- grad_sky: float32 [4, 262144, 128], P('band', 'tile')
- grad_params: float32 [5, 256], replicated
The draws below stay inside these ranges and needn't reach their ends.
Inputs may be any that keep to these rules, and one draw needn't show every extreme that they name: `foot_owner`: in each aligned block of 1024 columns (the columns of one device's row blocks) no owner index appears more than 16 times, and some owner appears exactly 16 times in some blocks.
All inputs are finite; a program needn't handle non-finite values.
Results may differ from the reference program's by a relative error of at most 0.006.
Values may be sent and summed in bfloat16 or wider, within the bound.
No kernel may reach another device: no remote copies, remote signals or barrier semaphores. Data moves between devices by JAX's collectives and lax.ppermute only.
A program may use at most 64 MiB of HBM per device.

```python
import math
import jax
import jax.numpy as jnp
import numpy as np
from jax import lax

COLS = 1024
BLOCK_ROWS = 128
TAPS = 25
COMPS = 4
EXPO = 256
RB_DEV = 1
SEG_DEV = 2048
NSTRIP = 4
NRB = 128
NSEG = 262144
CAP = 16
N_TILE = 128


def plant(values, own_key, smallest, high):
    longest = values.shape.index(max(values.shape))
    spots = []
    for shift in (0, 1):
        where = [jax.random.randint(jax.random.fold_in(own_key, axis), (), 0, length) for axis, length in enumerate(values.shape)]
        where[longest] = (where[longest] + shift) % values.shape[longest]
        spots.append(tuple(where))
    return values.at[spots[0]].set(smallest).at[spots[1]].set(high)


def levels(key, dims, shards, least, top_value):
    gain = 1.0
    for dim, shards_of in shards:
        draws = jax.random.uniform(jax.random.fold_in(jax.random.fold_in(key, 6), dim), (shards_of,), jnp.float32, least / len(shards), top_value / len(shards))
        gain = gain * jnp.repeat(jnp.exp(draws), dims[dim] // shards_of).reshape((-1,) + (1,) * (len(dims) - 1 - dim))
    return gain


def assign_block(key, own, number, rows, amount, top, limit, lean):
    order = jax.random.permutation(key, amount)
    crowded, ordinary = portions_of(amount, rows * top, limit, lean, True), portions_of(amount, rows * top, limit, lean, False)
    places = jnp.arange(amount)

    def named(tallies, turn):
        used = int((tallies > 0).sum())
        fixed = max(1, used // 4)
        passed = fixed + (places - fixed + turn * (used - fixed)) % max(1, amount - fixed)
        return jnp.zeros((amount,), jnp.int32).at[order[jnp.where(places < fixed, places, passed)]].set(jnp.asarray(tallies, jnp.int32))

    tallies = jnp.where(number % 4 == 0, named(crowded, number // 4), named(ordinary, number - number // 4 - 1))
    mixed = jax.random.permutation(jax.random.fold_in(own, 3), amount)
    donor, taker = mixed[0:amount // 2 * 2:2], mixed[1:amount // 2 * 2:2]
    room = jnp.minimum(tallies[donor] - 1, limit - tallies[taker]) // 2
    room = jnp.where((donor == order[0]) | (taker == order[0]) | (tallies[taker] == 0), 0, jnp.maximum(room, 0))
    passed = jax.random.randint(jax.random.fold_in(own, 4), (amount // 2,), 0, 1 << 20) % (room + 1)
    tallies = tallies.at[donor].add(-passed).at[taker].add(passed)
    items = jnp.searchsorted(jnp.cumsum(tallies), jnp.arange(rows * top), side="right").astype(jnp.int32)
    grid = items.reshape(top, rows).T
    grid = grid[jax.random.permutation(jax.random.fold_in(own, 1), rows)]
    turn = jax.random.randint(jax.random.fold_in(own, 2), (rows, 1), 0, top)
    return jnp.take_along_axis(grid, (jnp.arange(top)[None, :] + turn) % top, axis=1)


def portions_of(count, total, reach, skew, full):
    portions = [(1 << 20) // math.isqrt(standing ** skew) + 1 for standing in range(1, count + 1)]
    largest = reach if full else min(reach, max(-(-total // count), total * portions[0] // sum(portions)))
    least = 1 if total - largest >= count - 1 else 0
    counts, spare = [largest] + [least] * (count - 1), total - largest - least * (count - 1)
    while spare > 0:
        candidates = [i for i in range(1, count) if counts[i] < largest] or [i for i in range(1, count) if counts[i] < reach]
        pool, left = sum([portions[i] for i in candidates]), spare
        for i in candidates:
            extra = min(reach - counts[i], max(1, left * portions[i] // pool), spare)
            counts[i] = counts[i] + extra
            spare = spare - extra
    return np.array(counts)


def centred(stream_key, dims, deviation, reach, shards=(), kind=jnp.bfloat16):
    gain = levels(stream_key, dims, shards, -0.22, 0.18) if shards else 1.0
    array = jax.random.normal(stream_key, dims, jnp.float32) * deviation * gain
    return jnp.minimum(jnp.maximum(array, -reach), reach).astype(kind)


def setup_inputs(seed: int = 0) -> dict:
    key_of = jax.random.split(jax.random.key(seed), 12)
    sky_model = centred(key_of[0], (NSTRIP, NSEG, BLOCK_ROWS), 1.0, 6.0, ((0, 4), (1, 128)))
    observed = centred(key_of[1], (NSTRIP, NRB, COLS, BLOCK_ROWS), 1.0, 6.0, ((0, 4), (1, 128)))
    row_weight = jnp.clip(jnp.exp(math.log(1.0) - 2.3025851 * jax.random.uniform(key_of[2], (NSTRIP, NRB, BLOCK_ROWS), jnp.float32) ** levels(key_of[2], (NSTRIP, NRB, BLOCK_ROWS), ((0, 4), (1, 128)), -0.2, 0.2)), 0.1, 1.0)
    foot_owner_keys = jax.random.split(jax.random.fold_in(key_of[3], 1), NSTRIP * NRB * COLS // (RB_DEV * COLS))
    foot_owner_turns = jax.random.permutation(jax.random.fold_in(key_of[3], 3), NSTRIP * NRB * COLS // (RB_DEV * COLS))
    foot_owner = jax.vmap(lambda own, number: assign_block(jax.random.fold_in(key_of[3], 2), own, number, RB_DEV * COLS, N_TILE, 1, CAP, 2))(foot_owner_keys, foot_owner_turns).reshape((NSTRIP, NRB, COLS, 1))
    foot_local = plant(jax.random.randint(key_of[4], (NSTRIP, NRB, COLS), 0, SEG_DEV), jax.random.fold_in(key_of[4], 1), 0, SEG_DEV - 1).astype(jnp.int32)
    row_offset = plant(jax.random.randint(key_of[5], (NSTRIP, NRB), -4, 5), jax.random.fold_in(key_of[5], 1), -4, 4).astype(jnp.int32)
    exposure_of = plant(jax.random.randint(key_of[6], (NSTRIP, NRB), 0, EXPO), jax.random.fold_in(key_of[6], 1), 0, EXPO - 1).astype(jnp.int32)
    amplitude = jnp.clip(jnp.exp(jax.random.uniform(key_of[7], (COMPS, EXPO), jnp.float32, math.log(0.25), math.log(1.0))), 0.25, 1.0)
    subpixel_shift = jnp.clip(jax.random.uniform(key_of[8], (EXPO,), jnp.float32, 0.05, 0.95), 0.05, 0.95)
    column_profile = jnp.clip(jax.random.uniform(key_of[9], (EXPO, COMPS, TAPS), jnp.float32, 0.05, 0.3), 0.05, 0.3)
    row_profile = jnp.clip(jax.random.uniform(key_of[10], (EXPO, COMPS, TAPS), jnp.float32, 0.05, 0.3), 0.05, 0.3)
    return dict(sky_model=sky_model, observed=observed, row_weight=row_weight, foot_owner=foot_owner, foot_local=foot_local, row_offset=row_offset, exposure_of=exposure_of, amplitude=amplitude, subpixel_shift=subpixel_shift, column_profile=column_profile, row_profile=row_profile)


def band_matrix(profile, size):
    taps = profile.shape[-1]
    out_index = jnp.arange(size, dtype=jnp.int32)[:, None]
    in_index = jnp.arange(size, dtype=jnp.int32)[None, :]
    lag = in_index - out_index + taps // 2
    inside = (lag >= 0) & (lag < taps)
    picked = profile[..., jnp.clip(lag, 0, taps - 1)]
    return jnp.where(inside, picked, jnp.zeros_like(picked))


def one_block(inputs):
    fetched, observed_block, weight_rows, offset, frac, amps, wide_profile, tall_profile = inputs
    width = fetched.shape[0]
    rows = fetched.shape[1]
    pixels = width * rows
    j_index = jnp.arange(rows, dtype=jnp.int32)[:, None]
    v_index = jnp.arange(rows, dtype=jnp.int32)[None, :]
    lower_hit = j_index == v_index + offset
    upper_hit = j_index == v_index + offset + 1
    zero_b = jnp.zeros((), jnp.bfloat16)
    weight_low = (1.0 - frac).astype(jnp.bfloat16)
    weight_high = frac.astype(jnp.bfloat16)
    interp = jnp.where(lower_hit, weight_low, zero_b) + jnp.where(upper_hit, weight_high, zero_b)
    slope_map = upper_hit.astype(jnp.float32) - lower_hit.astype(jnp.float32)
    resampled = jnp.dot(fetched, interp, preferred_element_type=jnp.float32).astype(jnp.bfloat16)
    tall = band_matrix(lax.optimization_barrier(tall_profile.astype(jnp.bfloat16)), rows).astype(jnp.float32)
    wide = band_matrix(lax.optimization_barrier(wide_profile.astype(jnp.bfloat16)), width).astype(jnp.float32)
    blurred = jnp.einsum('uw,qvw->quv', resampled.astype(jnp.float32), tall).astype(jnp.bfloat16)
    component = jnp.einsum('qux,qxv->quv', wide, blurred.astype(jnp.float32))
    model = jnp.sum(amps[:, None, None] * component, axis=0)
    weighted = weight_rows[None, :] * (model - observed_block.astype(jnp.float32))
    amp_term = jnp.sum(component * weighted[None], axis=(1, 2)) / pixels
    residual_b = weighted.astype(jnp.bfloat16)
    back_wide = jnp.einsum('qxu,xv->quv', wide, residual_b.astype(jnp.float32)).astype(jnp.bfloat16)
    image_adjoint = jnp.sum(amps[:, None, None] * jnp.einsum('quv,qvw->quw', back_wide.astype(jnp.float32), tall), axis=0)
    adjoint_b = image_adjoint.astype(jnp.bfloat16)
    slope = jnp.dot(fetched.astype(jnp.float32), slope_map, precision=lax.Precision.HIGHEST)
    shift_term = jnp.sum(image_adjoint * slope) / pixels
    segment_grad = jnp.dot(adjoint_b, interp.T, preferred_element_type=jnp.float32)
    return segment_grad, amp_term, shift_term


def reference(sky_model, observed, row_weight, foot_owner, foot_local, row_offset, exposure_of, amplitude, subpixel_shift, column_profile, row_profile):
    strips = sky_model.shape[0]
    seg_total = sky_model.shape[1]
    rows = sky_model.shape[2]
    block_total = observed.shape[1]
    width = observed.shape[2]
    seg_index = foot_owner[..., 0] * SEG_DEV + foot_local
    strip_base = (jnp.arange(strips, dtype=jnp.int32) * seg_total)[:, None, None]
    global_index = (seg_index + strip_base).astype(jnp.int32).reshape(strips * block_total, width)
    flat_sky = sky_model.reshape(strips * seg_total, rows)
    expo_flat = exposure_of.reshape(strips * block_total).astype(jnp.int32)

    def per_block(items):
        index_row, observed_block, weight_rows, offset, expo = items
        fetched = jnp.take(flat_sky, index_row, axis=0)
        return one_block((fetched, observed_block, weight_rows, offset, subpixel_shift[expo], amplitude[:, expo], column_profile[expo], row_profile[expo]))

    segment_grad, amp_term, shift_term = lax.map(per_block, (global_index, observed.reshape(strips * block_total, width, rows), row_weight.reshape(strips * block_total, rows), row_offset.reshape(strips * block_total).astype(jnp.int32), expo_flat))
    grad_flat = jnp.zeros((strips * seg_total, rows), jnp.float32).at[global_index.reshape(-1)].add(segment_grad.reshape(-1, rows))
    grad_sky = grad_flat.reshape(strips, seg_total, rows)
    amp_sums = jax.ops.segment_sum(amp_term, expo_flat, num_segments=EXPO)
    shift_sums = jax.ops.segment_sum(shift_term, expo_flat, num_segments=EXPO)
    grad_params = jnp.concatenate([amp_sums.T, shift_sums[None, :]], axis=0)
    return grad_sky, grad_params
```

```python
import jax
import jax.numpy as jnp
from jax import lax
from jax.sharding import PartitionSpec as P


def band_lookup(profile, lag_shift, size):
    taps = profile.shape[-1]
    out_index = jnp.arange(size, dtype=jnp.int32)[:, None]
    in_index = jnp.arange(size, dtype=jnp.int32)[None, :]
    lag = in_index - out_index + taps // 2 + lag_shift
    tap_mask = (lag[:, :, None] == jnp.arange(taps, dtype=jnp.int32)[None, None, :]).astype(
        jnp.bfloat16
    )
    return jnp.einsum(
        "vwt,bqt->bqvw", tap_mask, profile, preferred_element_type=jnp.float32
    ).astype(jnp.bfloat16)


def from_previous(values):
    blank = jnp.zeros_like(values[:, :, :1])
    return jnp.concatenate([blank, values[:, :, :-1]], axis=2)


def from_next(values):
    blank = jnp.zeros_like(values[:, :, :1])
    return jnp.concatenate([values[:, :, 1:], blank], axis=2)


def strict_lower(size):
    above = jnp.arange(size, dtype=jnp.int32)[:, None]
    below = jnp.arange(size, dtype=jnp.int32)[None, :]
    return (below < above).astype(jnp.bfloat16)


def body(
    sky_model,
    observed,
    row_weight,
    foot_owner,
    foot_local,
    row_offset,
    exposure_of,
    amplitude,
    subpixel_shift,
    column_profile,
    row_profile,
):
    tile_count = lax.axis_size("tile")
    seg_count = sky_model.shape[1]
    block_rows = sky_model.shape[2]
    block_count = observed.shape[1]
    width = observed.shape[2]
    capacity = 2 * block_count * width // tile_count
    expo_count = amplitude.shape[1]
    comp_count = amplitude.shape[0]
    tile_blocks = width // block_rows
    requests = block_count * width
    pixels = width * block_rows
    highest = lax.Precision.HIGHEST
    bfloat = jnp.bfloat16
    single = jnp.float32
    request_owner = foot_owner.reshape(requests)
    request_local = foot_local.reshape(requests)
    owner_hits = (
        request_owner.reshape(block_count, width)[:, :, None]
        == jnp.arange(tile_count, dtype=jnp.int32)[None, None, :]
    )
    owner_onehot = owner_hits.astype(bfloat)
    within = jnp.einsum(
        "uy,byt->but", strict_lower(width), owner_onehot, preferred_element_type=single
    )
    block_totals = jnp.sum(owner_onehot.astype(single), axis=1)
    before = jnp.dot(strict_lower(block_count).astype(single), block_totals, precision=highest)
    rank_table = jnp.where(owner_hits, within + before[:, None, :], jnp.zeros((), single))
    owner_rank = jnp.sum(rank_table, axis=2).astype(jnp.int32).reshape(requests)
    slot_index = request_owner * capacity + owner_rank
    empty_ids = jnp.zeros((tile_count * capacity,), jnp.int32)
    request_ids = empty_ids.at[slot_index].set(request_local + 1).reshape(tile_count, capacity)
    block_offset = row_offset.reshape(block_count)
    block_exposure = exposure_of.reshape(block_count)
    served_ids = lax.all_to_all(request_ids, "tile", split_axis=0, concat_axis=0, tiled=True)
    served_valid = served_ids > 0
    served_where = jnp.maximum(served_ids - 1, 0)
    local_sky = sky_model[0]
    picked_rows = jnp.take(local_sky, served_where.reshape(tile_count * capacity), axis=0)
    picked_rows = jnp.where(
        served_valid.reshape(tile_count * capacity)[:, None],
        picked_rows,
        jnp.zeros_like(picked_rows),
    )
    served_rows = picked_rows.reshape(tile_count, capacity, block_rows)
    returned = lax.all_to_all(served_rows, "tile", split_axis=0, concat_axis=0, tiled=True)
    fetched = jnp.take(
        returned.reshape(tile_count * capacity, block_rows), slot_index, axis=0
    ).reshape(block_count, width, block_rows)
    expo_onehot = (
        block_exposure[:, None] == jnp.arange(expo_count, dtype=jnp.int32)[None, :]
    ).astype(single)
    block_amp = jnp.dot(expo_onehot, amplitude.T, precision=highest)
    block_frac = jnp.dot(expo_onehot, subpixel_shift, precision=highest)
    block_wide = jnp.einsum("be,eqt->bqt", expo_onehot, column_profile, precision=highest)
    block_tall = jnp.einsum("be,eqt->bqt", expo_onehot, row_profile, precision=highest)
    j_index = jnp.arange(block_rows, dtype=jnp.int32)[None, :, None]
    v_index = jnp.arange(block_rows, dtype=jnp.int32)[None, None, :]
    offsets = block_offset[:, None, None]
    lower_hit = j_index == v_index + offsets
    upper_hit = j_index == v_index + offsets + 1
    zero_b = jnp.zeros((), bfloat)
    weight_low = (1.0 - block_frac).astype(bfloat)[:, None, None]
    weight_high = block_frac.astype(bfloat)[:, None, None]
    interp = jnp.where(lower_hit, weight_low, zero_b) + jnp.where(upper_hit, weight_high, zero_b)
    slope_map = upper_hit.astype(bfloat) - lower_hit.astype(bfloat)
    tall_kernel = band_lookup(block_tall.astype(bfloat), 0, block_rows)
    wide_profile_b = block_wide.astype(bfloat)
    wide_main = band_lookup(wide_profile_b, 0, block_rows)
    wide_prev = band_lookup(wide_profile_b, -block_rows, block_rows)
    wide_next = band_lookup(wide_profile_b, block_rows, block_rows)
    resampled = jnp.einsum("buj,bjv->buv", fetched, interp, preferred_element_type=single).astype(
        bfloat
    )
    blurred = jnp.einsum(
        "buw,bqvw->bquv", resampled, tall_kernel, preferred_element_type=single
    ).astype(bfloat)
    blurred_tiles = blurred.reshape(block_count, comp_count, tile_blocks, block_rows, block_rows)
    component = jnp.einsum(
        "bqxy,bqiyv->bqixv", wide_main, blurred_tiles, preferred_element_type=single
    )
    component = component + from_previous(
        jnp.einsum("bqxy,bqiyv->bqixv", wide_prev, blurred_tiles, preferred_element_type=single)
    )
    component = component + from_next(
        jnp.einsum("bqxy,bqiyv->bqixv", wide_next, blurred_tiles, preferred_element_type=single)
    )
    component = component.reshape(block_count, comp_count, width, block_rows)
    model = jnp.sum(block_amp[:, :, None, None] * component, axis=1)
    weighted = row_weight.reshape(block_count, block_rows)[:, None, :] * (
        model - observed[0].astype(single)
    )
    amp_term = jnp.sum(component * weighted[:, None], axis=(2, 3)) / pixels
    residual_b = weighted.astype(bfloat)
    residual_tiles = residual_b.reshape(block_count, tile_blocks, block_rows, block_rows)
    back_wide = jnp.einsum(
        "bqyx,biyv->bqixv", wide_main, residual_tiles, preferred_element_type=single
    )
    back_wide = back_wide + from_next(
        jnp.einsum("bqyx,biyv->bqixv", wide_prev, residual_tiles, preferred_element_type=single)
    )
    back_wide = back_wide + from_previous(
        jnp.einsum("bqyx,biyv->bqixv", wide_next, residual_tiles, preferred_element_type=single)
    )
    back_wide = back_wide.reshape(block_count, comp_count, width, block_rows).astype(bfloat)
    image_adjoint = jnp.sum(
        block_amp[:, :, None, None]
        * jnp.einsum("bquv,bqvw->bquw", back_wide, tall_kernel, preferred_element_type=single),
        axis=1,
    )
    adjoint_b = image_adjoint.astype(bfloat)
    slope = jnp.einsum("buj,bjv->buv", fetched, slope_map, preferred_element_type=single)
    shift_term = jnp.sum(image_adjoint * slope, axis=(1, 2)) / pixels
    block_terms = jnp.concatenate([amp_term, shift_term[:, None]], axis=1)
    term_count = comp_count + 1
    terms_high = lax.reduce_precision(block_terms, exponent_bits=8, mantissa_bits=7)
    terms_low = block_terms - terms_high
    term_row = jnp.concatenate(
        [
            terms_high.astype(bfloat),
            terms_low.astype(bfloat),
            block_exposure.astype(bfloat)[:, None],
        ],
        axis=1,
    ).reshape(block_count * (2 * term_count + 1))
    term_row = jnp.pad(term_row, (0, block_rows - term_row.shape[0]))
    segment_grad = jnp.einsum("buv,bjv->buj", adjoint_b, interp, preferred_element_type=single)
    send_grad = (
        jnp.zeros((tile_count * capacity, block_rows), single)
        .at[slot_index]
        .set(segment_grad.reshape(requests, block_rows))
        .reshape(tile_count, capacity, block_rows)
    )
    send_all = jnp.concatenate(
        [
            send_grad.astype(bfloat),
            jnp.broadcast_to(term_row[None, None, :], (tile_count, 1, block_rows)),
        ],
        axis=1,
    )
    received = lax.all_to_all(send_all, "tile", split_axis=0, concat_axis=0, tiled=True)
    segment_rows = received[:, :capacity].astype(single)
    peer_rows = received[:, capacity, : block_count * (2 * term_count + 1)].astype(single)
    peer_rows = peer_rows.reshape(tile_count * block_count, 2 * term_count + 1)
    peer_terms = peer_rows[:, :term_count] + peer_rows[:, term_count : 2 * term_count]
    peer_onehot = (
        peer_rows[:, 2 * term_count][:, None] == jnp.arange(expo_count, dtype=single)[None, :]
    ).astype(single)
    partial_params = jnp.dot(peer_terms.T, peer_onehot, precision=highest)
    flat_rows = segment_rows.reshape(tile_count * capacity, block_rows)
    flat_rows = jnp.where(
        served_valid.reshape(tile_count * capacity)[:, None], flat_rows, jnp.zeros_like(flat_rows)
    )
    grad_local = (
        jnp.zeros((seg_count, block_rows), single)
        .at[served_where.reshape(tile_count * capacity)]
        .add(flat_rows)
    )
    grad_params = lax.psum(partial_params, "band")
    return (grad_local[None], grad_params)


def solution(mesh):
    placed = (
        P("band", "tile", None),
        P("band", "tile", None, None),
        P("band", "tile", None),
        P("band", "tile", None, None),
        P("band", "tile", None),
        P("band", "tile"),
        P("band", "tile"),
        P(),
        P(),
        P(),
        P(),
    )
    return jax.shard_map(
        body, mesh=mesh, in_specs=placed, out_specs=(P("band", "tile", None), P()), check_vma=False
    )
```

```python
import jax
import jax.numpy as jnp
from jax import lax
from jax.sharding import PartitionSpec as P


def band_lookup(profile, lag_shift, size):
    taps = profile.shape[-1]
    out_index = jnp.arange(size, dtype=jnp.int32)[:, None]
    in_index = jnp.arange(size, dtype=jnp.int32)[None, :]
    lag = in_index - out_index + taps // 2 + lag_shift
    tap_mask = (lag[:, :, None] == jnp.arange(taps, dtype=jnp.int32)[None, None, :]).astype(
        jnp.bfloat16
    )
    return jnp.einsum(
        "vwt,bqt->bqvw", tap_mask, profile, preferred_element_type=jnp.float32
    ).astype(jnp.bfloat16)


def from_previous(values):
    blank = jnp.zeros_like(values[:, :, :1])
    return jnp.concatenate([blank, values[:, :, :-1]], axis=2)


def from_next(values):
    blank = jnp.zeros_like(values[:, :, :1])
    return jnp.concatenate([values[:, :, 1:], blank], axis=2)


def strict_lower(size):
    above = jnp.arange(size, dtype=jnp.int32)[:, None]
    below = jnp.arange(size, dtype=jnp.int32)[None, :]
    return (below < above).astype(jnp.bfloat16)


def body(
    sky_model,
    observed,
    row_weight,
    foot_owner,
    foot_local,
    row_offset,
    exposure_of,
    amplitude,
    subpixel_shift,
    column_profile,
    row_profile,
):
    tile_count = lax.axis_size("tile")
    seg_count = sky_model.shape[1]
    block_rows = sky_model.shape[2]
    block_count = observed.shape[1]
    width = observed.shape[2]
    capacity = 2 * block_count * width // tile_count
    expo_count = amplitude.shape[1]
    comp_count = amplitude.shape[0]
    tile_blocks = width // block_rows
    requests = block_count * width
    pixels = width * block_rows
    highest = lax.Precision.HIGHEST
    bfloat = jnp.bfloat16
    single = jnp.float32
    request_owner = foot_owner.reshape(requests)
    request_local = foot_local.reshape(requests)
    owner_hits = (
        request_owner.reshape(block_count, width)[:, :, None]
        == jnp.arange(tile_count, dtype=jnp.int32)[None, None, :]
    )
    owner_onehot = owner_hits.astype(bfloat)
    within = jnp.einsum(
        "uy,byt->but", strict_lower(width), owner_onehot, preferred_element_type=single
    )
    block_totals = jnp.sum(owner_onehot.astype(single), axis=1)
    before = jnp.dot(strict_lower(block_count).astype(single), block_totals, precision=highest)
    rank_table = jnp.where(owner_hits, within + before[:, None, :], jnp.zeros((), single))
    owner_rank = jnp.sum(rank_table, axis=2).astype(jnp.int32).reshape(requests)
    slot_index = request_owner * capacity + owner_rank
    empty_ids = jnp.zeros((tile_count * capacity,), jnp.int32)
    request_ids = empty_ids.at[slot_index].set(request_local + 1).reshape(tile_count, capacity)
    block_offset = row_offset.reshape(block_count)
    block_exposure = exposure_of.reshape(block_count)
    served_ids = lax.all_to_all(request_ids, "tile", split_axis=0, concat_axis=0, tiled=True)
    served_valid = served_ids > 0
    served_where = jnp.maximum(served_ids - 1, 0)
    local_sky = sky_model[0]
    served_flat = served_ids.reshape(tile_count * capacity) - 1
    seg_iota = jnp.arange(seg_count, dtype=jnp.int32)
    serve_onehot = (served_flat[:, None] == seg_iota[None, :]).astype(bfloat)
    picked_rows = jnp.dot(serve_onehot, local_sky, preferred_element_type=single).astype(bfloat)
    served_rows = picked_rows.reshape(tile_count, capacity, block_rows)
    returned = lax.all_to_all(served_rows, "tile", split_axis=0, concat_axis=0, tiled=True)
    slot_iota = jnp.arange(tile_count * capacity, dtype=jnp.int32)
    slot_onehot = (slot_index[:, None] == slot_iota[None, :]).astype(bfloat)
    fetched = (
        jnp.dot(
            slot_onehot,
            returned.reshape(tile_count * capacity, block_rows),
            preferred_element_type=single,
        )
        .astype(bfloat)
        .reshape(block_count, width, block_rows)
    )
    expo_onehot = (
        block_exposure[:, None] == jnp.arange(expo_count, dtype=jnp.int32)[None, :]
    ).astype(single)
    block_amp = jnp.dot(expo_onehot, amplitude.T, precision=highest)
    block_frac = jnp.dot(expo_onehot, subpixel_shift, precision=highest)
    block_wide = jnp.einsum("be,eqt->bqt", expo_onehot, column_profile, precision=highest)
    block_tall = jnp.einsum("be,eqt->bqt", expo_onehot, row_profile, precision=highest)
    j_index = jnp.arange(block_rows, dtype=jnp.int32)[None, :, None]
    v_index = jnp.arange(block_rows, dtype=jnp.int32)[None, None, :]
    offsets = block_offset[:, None, None]
    lower_hit = j_index == v_index + offsets
    upper_hit = j_index == v_index + offsets + 1
    zero_b = jnp.zeros((), bfloat)
    weight_low = (1.0 - block_frac).astype(bfloat)[:, None, None]
    weight_high = block_frac.astype(bfloat)[:, None, None]
    interp = jnp.where(lower_hit, weight_low, zero_b) + jnp.where(upper_hit, weight_high, zero_b)
    slope_map = upper_hit.astype(bfloat) - lower_hit.astype(bfloat)
    tall_kernel = band_lookup(block_tall.astype(bfloat), 0, block_rows)
    wide_profile_b = block_wide.astype(bfloat)
    wide_main = band_lookup(wide_profile_b, 0, block_rows)
    wide_prev = band_lookup(wide_profile_b, -block_rows, block_rows)
    wide_next = band_lookup(wide_profile_b, block_rows, block_rows)
    resampled = jnp.einsum("buj,bjv->buv", fetched, interp, preferred_element_type=single).astype(
        bfloat
    )
    blurred = jnp.einsum(
        "buw,bqvw->bquv", resampled, tall_kernel, preferred_element_type=single
    ).astype(bfloat)
    blurred_tiles = blurred.reshape(block_count, comp_count, tile_blocks, block_rows, block_rows)
    component = jnp.einsum(
        "bqxy,bqiyv->bqixv", wide_main, blurred_tiles, preferred_element_type=single
    )
    component = component + from_previous(
        jnp.einsum("bqxy,bqiyv->bqixv", wide_prev, blurred_tiles, preferred_element_type=single)
    )
    component = component + from_next(
        jnp.einsum("bqxy,bqiyv->bqixv", wide_next, blurred_tiles, preferred_element_type=single)
    )
    component = component.reshape(block_count, comp_count, width, block_rows)
    model = jnp.sum(block_amp[:, :, None, None] * component, axis=1)
    weighted = row_weight.reshape(block_count, block_rows)[:, None, :] * (
        model - observed[0].astype(single)
    )
    amp_term = jnp.sum(component * weighted[:, None], axis=(2, 3)) / pixels
    residual_b = weighted.astype(bfloat)
    residual_tiles = residual_b.reshape(block_count, tile_blocks, block_rows, block_rows)
    back_wide = jnp.einsum(
        "bqyx,biyv->bqixv", wide_main, residual_tiles, preferred_element_type=single
    )
    back_wide = back_wide + from_next(
        jnp.einsum("bqyx,biyv->bqixv", wide_prev, residual_tiles, preferred_element_type=single)
    )
    back_wide = back_wide + from_previous(
        jnp.einsum("bqyx,biyv->bqixv", wide_next, residual_tiles, preferred_element_type=single)
    )
    back_wide = back_wide.reshape(block_count, comp_count, width, block_rows).astype(bfloat)
    image_adjoint = jnp.sum(
        block_amp[:, :, None, None]
        * jnp.einsum("bquv,bqvw->bquw", back_wide, tall_kernel, preferred_element_type=single),
        axis=1,
    )
    adjoint_b = image_adjoint.astype(bfloat)
    slope = jnp.einsum("buj,bjv->buv", fetched, slope_map, preferred_element_type=single)
    shift_term = jnp.sum(image_adjoint * slope, axis=(1, 2)) / pixels
    block_terms = jnp.concatenate([amp_term, shift_term[:, None]], axis=1)
    term_count = comp_count + 1
    terms_high = lax.reduce_precision(block_terms, exponent_bits=8, mantissa_bits=7)
    terms_low = block_terms - terms_high
    term_row = jnp.concatenate(
        [
            terms_high.astype(bfloat),
            terms_low.astype(bfloat),
            block_exposure.astype(bfloat)[:, None],
        ],
        axis=1,
    ).reshape(block_count * (2 * term_count + 1))
    term_row = jnp.pad(term_row, (0, block_rows - term_row.shape[0]))
    segment_grad = jnp.einsum("buv,bjv->buj", adjoint_b, interp, preferred_element_type=single)
    send_grad = (
        jnp.einsum(
            "us,uj->sj",
            slot_onehot,
            segment_grad.reshape(requests, block_rows).astype(bfloat),
            preferred_element_type=single,
        )
        .astype(bfloat)
        .reshape(tile_count, capacity, block_rows)
    )
    send_all = jnp.concatenate(
        [
            send_grad.astype(bfloat),
            jnp.broadcast_to(term_row[None, None, :], (tile_count, 1, block_rows)),
        ],
        axis=1,
    )
    received = lax.all_to_all(send_all, "tile", split_axis=0, concat_axis=0, tiled=True)
    segment_rows = received[:, :capacity]
    peer_rows = received[:, capacity, : block_count * (2 * term_count + 1)].astype(single)
    peer_rows = peer_rows.reshape(tile_count * block_count, 2 * term_count + 1)
    peer_terms = peer_rows[:, :term_count] + peer_rows[:, term_count : 2 * term_count]
    peer_onehot = (
        peer_rows[:, 2 * term_count][:, None] == jnp.arange(expo_count, dtype=single)[None, :]
    ).astype(single)
    partial_params = jnp.dot(peer_terms.T, peer_onehot, precision=highest)
    flat_rows = segment_rows.reshape(tile_count * capacity, block_rows)
    grad_local = jnp.einsum(
        "ik,ij->kj", serve_onehot, flat_rows, preferred_element_type=single
    )
    grad_params = lax.psum(partial_params, "band")
    return (grad_local[None], grad_params)


def solution(mesh):
    placed = (
        P("band", "tile", None),
        P("band", "tile", None, None),
        P("band", "tile", None),
        P("band", "tile", None, None),
        P("band", "tile", None),
        P("band", "tile"),
        P("band", "tile"),
        P(),
        P(),
        P(),
        P(),
    )
    return jax.shard_map(
        body, mesh=mesh, in_specs=placed, out_specs=(P("band", "tile", None), P()), check_vma=False
    )
```

```python
import jax
import jax.numpy as jnp
from jax import lax
from jax.sharding import PartitionSpec as P


def band_lookup(profile, lag_shift, size):
    taps = profile.shape[-1]
    out_index = jnp.arange(size, dtype=jnp.int32)[:, None]
    in_index = jnp.arange(size, dtype=jnp.int32)[None, :]
    lag = in_index - out_index + taps // 2 + lag_shift
    tap_mask = (lag[:, :, None] == jnp.arange(taps, dtype=jnp.int32)[None, None, :]).astype(
        jnp.bfloat16
    )
    return jnp.einsum(
        "vwt,bqt->bqvw", tap_mask, profile, preferred_element_type=jnp.float32
    ).astype(jnp.bfloat16)


def from_previous(values):
    blank = jnp.zeros_like(values[:, :, :1])
    return jnp.concatenate([blank, values[:, :, :-1]], axis=2)


def from_next(values):
    blank = jnp.zeros_like(values[:, :, :1])
    return jnp.concatenate([values[:, :, 1:], blank], axis=2)


def strict_lower(size):
    above = jnp.arange(size, dtype=jnp.int32)[:, None]
    below = jnp.arange(size, dtype=jnp.int32)[None, :]
    return (below < above).astype(jnp.bfloat16)


def body(
    sky_model,
    observed,
    row_weight,
    foot_owner,
    foot_local,
    row_offset,
    exposure_of,
    amplitude,
    subpixel_shift,
    column_profile,
    row_profile,
):
    tile_count = lax.axis_size("tile")
    seg_count = sky_model.shape[1]
    block_rows = sky_model.shape[2]
    block_count = observed.shape[1]
    width = observed.shape[2]
    capacity = 2 * block_count * width // tile_count
    expo_count = amplitude.shape[1]
    comp_count = amplitude.shape[0]
    tile_blocks = width // block_rows
    requests = block_count * width
    pixels = width * block_rows
    highest = lax.Precision.HIGHEST
    bfloat = jnp.bfloat16
    single = jnp.float32
    request_owner = foot_owner.reshape(requests)
    request_local = foot_local.reshape(requests)
    owner_hits = (
        request_owner.reshape(block_count, width)[:, :, None]
        == jnp.arange(tile_count, dtype=jnp.int32)[None, None, :]
    )
    owner_onehot = owner_hits.astype(bfloat)
    within = jnp.einsum(
        "uy,byt->but", strict_lower(width), owner_onehot, preferred_element_type=single
    )
    block_totals = jnp.sum(owner_onehot.astype(single), axis=1)
    before = jnp.dot(strict_lower(block_count).astype(single), block_totals, precision=highest)
    rank_table = jnp.where(owner_hits, within + before[:, None, :], jnp.zeros((), single))
    owner_rank = jnp.sum(rank_table, axis=2).astype(jnp.int32).reshape(requests)
    slot_index = request_owner * capacity + owner_rank
    slot_iota = jnp.arange(tile_count * capacity, dtype=jnp.int32)
    slot_onehot_t = (slot_iota[:, None] == slot_index[None, :]).astype(bfloat)
    request_code = request_local + 1
    request_parts = jnp.stack([request_code // 32, request_code % 32], axis=1).astype(bfloat)
    request_sums = jnp.dot(slot_onehot_t, request_parts, preferred_element_type=single)
    request_ids = (
        request_sums[:, 0].astype(jnp.int32) * 32 + request_sums[:, 1].astype(jnp.int32)
    ).reshape(tile_count, capacity)
    block_offset = row_offset.reshape(block_count)
    block_exposure = exposure_of.reshape(block_count)
    served_ids = lax.all_to_all(request_ids, "tile", split_axis=0, concat_axis=0, tiled=True)
    served_valid = served_ids > 0
    served_where = jnp.maximum(served_ids - 1, 0)
    local_sky = sky_model[0]
    served_flat = served_ids.reshape(tile_count * capacity) - 1
    seg_iota = jnp.arange(seg_count, dtype=jnp.int32)
    serve_onehot = (served_flat[:, None] == seg_iota[None, :]).astype(bfloat)
    picked_rows = jnp.dot(serve_onehot, local_sky, preferred_element_type=single).astype(bfloat)
    served_rows = picked_rows.reshape(tile_count, capacity, block_rows)
    returned = lax.all_to_all(served_rows, "tile", split_axis=0, concat_axis=0, tiled=True)
    slot_onehot = (slot_index[:, None] == slot_iota[None, :]).astype(bfloat)
    fetched = (
        jnp.dot(
            slot_onehot,
            returned.reshape(tile_count * capacity, block_rows),
            preferred_element_type=single,
        )
        .astype(bfloat)
        .reshape(block_count, width, block_rows)
    )
    expo_onehot = (
        block_exposure[:, None] == jnp.arange(expo_count, dtype=jnp.int32)[None, :]
    ).astype(single)
    block_amp = jnp.dot(expo_onehot, amplitude.T, precision=highest)
    block_frac = jnp.dot(expo_onehot, subpixel_shift, precision=highest)
    block_wide = jnp.einsum("be,eqt->bqt", expo_onehot, column_profile, precision=highest)
    block_tall = jnp.einsum("be,eqt->bqt", expo_onehot, row_profile, precision=highest)
    j_index = jnp.arange(block_rows, dtype=jnp.int32)[None, :, None]
    v_index = jnp.arange(block_rows, dtype=jnp.int32)[None, None, :]
    offsets = block_offset[:, None, None]
    lower_hit = j_index == v_index + offsets
    upper_hit = j_index == v_index + offsets + 1
    zero_b = jnp.zeros((), bfloat)
    weight_low = (1.0 - block_frac).astype(bfloat)[:, None, None]
    weight_high = block_frac.astype(bfloat)[:, None, None]
    interp = jnp.where(lower_hit, weight_low, zero_b) + jnp.where(upper_hit, weight_high, zero_b)
    slope_map = upper_hit.astype(bfloat) - lower_hit.astype(bfloat)
    tall_kernel = band_lookup(block_tall.astype(bfloat), 0, block_rows)
    wide_profile_b = block_wide.astype(bfloat)
    wide_main = band_lookup(wide_profile_b, 0, block_rows)
    wide_prev = band_lookup(wide_profile_b, -block_rows, block_rows)
    wide_next = band_lookup(wide_profile_b, block_rows, block_rows)
    resampled = jnp.einsum("buj,bjv->buv", fetched, interp, preferred_element_type=single).astype(
        bfloat
    )
    blurred = jnp.einsum(
        "buw,bqvw->bquv", resampled, tall_kernel, preferred_element_type=single
    ).astype(bfloat)
    blurred_tiles = blurred.reshape(block_count, comp_count, tile_blocks, block_rows, block_rows)
    component = jnp.einsum(
        "bqxy,bqiyv->bqixv", wide_main, blurred_tiles, preferred_element_type=single
    )
    component = component + from_previous(
        jnp.einsum("bqxy,bqiyv->bqixv", wide_prev, blurred_tiles, preferred_element_type=single)
    )
    component = component + from_next(
        jnp.einsum("bqxy,bqiyv->bqixv", wide_next, blurred_tiles, preferred_element_type=single)
    )
    component = component.reshape(block_count, comp_count, width, block_rows)
    model = jnp.sum(block_amp[:, :, None, None] * component, axis=1)
    weighted = row_weight.reshape(block_count, block_rows)[:, None, :] * (
        model - observed[0].astype(single)
    )
    amp_term = jnp.sum(component * weighted[:, None], axis=(2, 3)) / pixels
    residual_b = weighted.astype(bfloat)
    residual_tiles = residual_b.reshape(block_count, tile_blocks, block_rows, block_rows)
    back_wide = jnp.einsum(
        "bqyx,biyv->bqixv", wide_main, residual_tiles, preferred_element_type=single
    )
    back_wide = back_wide + from_next(
        jnp.einsum("bqyx,biyv->bqixv", wide_prev, residual_tiles, preferred_element_type=single)
    )
    back_wide = back_wide + from_previous(
        jnp.einsum("bqyx,biyv->bqixv", wide_next, residual_tiles, preferred_element_type=single)
    )
    back_wide = back_wide.reshape(block_count, comp_count, width, block_rows).astype(bfloat)
    image_adjoint = jnp.sum(
        block_amp[:, :, None, None]
        * jnp.einsum("bquv,bqvw->bquw", back_wide, tall_kernel, preferred_element_type=single),
        axis=1,
    )
    adjoint_b = image_adjoint.astype(bfloat)
    slope = jnp.einsum("buj,bjv->buv", fetched, slope_map, preferred_element_type=single)
    shift_term = jnp.sum(image_adjoint * slope, axis=(1, 2)) / pixels
    block_terms = jnp.concatenate([amp_term, shift_term[:, None]], axis=1)
    term_count = comp_count + 1
    terms_high = lax.reduce_precision(block_terms, exponent_bits=8, mantissa_bits=7)
    terms_low = block_terms - terms_high
    term_row = jnp.concatenate(
        [
            terms_high.astype(bfloat),
            terms_low.astype(bfloat),
            block_exposure.astype(bfloat)[:, None],
        ],
        axis=1,
    ).reshape(block_count * (2 * term_count + 1))
    term_row = jnp.pad(term_row, (0, block_rows - term_row.shape[0]))
    segment_grad = jnp.einsum("buv,bjv->buj", adjoint_b, interp, preferred_element_type=single)
    send_grad = (
        jnp.dot(
            slot_onehot_t,
            segment_grad.reshape(requests, block_rows).astype(bfloat),
            preferred_element_type=single,
        )
        .astype(bfloat)
        .reshape(tile_count, capacity, block_rows)
    )
    send_all = jnp.concatenate(
        [
            send_grad.astype(bfloat),
            jnp.broadcast_to(term_row[None, None, :], (tile_count, 1, block_rows)),
        ],
        axis=1,
    )
    received = lax.all_to_all(send_all, "tile", split_axis=0, concat_axis=0, tiled=True)
    segment_rows = received[:, :capacity]
    peer_rows = received[:, capacity, : block_count * (2 * term_count + 1)].astype(single)
    peer_rows = peer_rows.reshape(tile_count * block_count, 2 * term_count + 1)
    peer_terms = peer_rows[:, :term_count] + peer_rows[:, term_count : 2 * term_count]
    peer_onehot = (
        peer_rows[:, 2 * term_count][:, None] == jnp.arange(expo_count, dtype=single)[None, :]
    ).astype(single)
    partial_params = jnp.dot(peer_terms.T, peer_onehot, precision=highest)
    flat_rows = segment_rows.reshape(tile_count * capacity, block_rows)
    serve_onehot_t = (seg_iota[:, None] == served_flat[None, :]).astype(bfloat)
    grad_local = jnp.dot(serve_onehot_t, flat_rows, preferred_element_type=single)
    grad_params = lax.psum(partial_params, "band")
    return (grad_local[None], grad_params)


def solution(mesh):
    placed = (
        P("band", "tile", None),
        P("band", "tile", None, None),
        P("band", "tile", None),
        P("band", "tile", None, None),
        P("band", "tile", None),
        P("band", "tile"),
        P("band", "tile"),
        P(),
        P(),
        P(),
        P(),
    )
    return jax.shard_map(
        body, mesh=mesh, in_specs=placed, out_specs=(P("band", "tile", None), P()), check_vma=False
    )
```

```python
import jax
import jax.numpy as jnp
from jax import lax
from jax.sharding import PartitionSpec as P
from jax.experimental import pallas as pl
from jax.experimental.pallas import tpu as pltpu


def band_lookup(profile, lag_shift, size):
    taps = profile.shape[-1]
    out_index = jnp.arange(size, dtype=jnp.int32)[:, None]
    in_index = jnp.arange(size, dtype=jnp.int32)[None, :]
    lag = in_index - out_index + taps // 2 + lag_shift
    tap_mask = (lag[:, :, None] == jnp.arange(taps, dtype=jnp.int32)[None, None, :]).astype(
        jnp.bfloat16
    )
    return jnp.einsum(
        "vwt,bqt->bqvw", tap_mask, profile, preferred_element_type=jnp.float32
    ).astype(jnp.bfloat16)


def from_previous(values):
    blank = jnp.zeros_like(values[:, :, :1])
    return jnp.concatenate([blank, values[:, :, :-1]], axis=2)


def from_next(values):
    blank = jnp.zeros_like(values[:, :, :1])
    return jnp.concatenate([values[:, :, 1:], blank], axis=2)


def strict_lower(size):
    above = jnp.arange(size, dtype=jnp.int32)[:, None]
    below = jnp.arange(size, dtype=jnp.int32)[None, :]
    return (below < above).astype(jnp.bfloat16)


def block_kernel(
    fetched_ref, observed_ref, weight_ref, amp_ref, interp_ref, interp_t_ref, slope_ref,
    tall_t_ref, tall_ref, main_ref, prev_ref, next_ref, main_t_ref, prev_t_ref, next_t_ref,
    grad_ref, terms_ref, comp_ref,
):
    single = jnp.float32
    bfloat = jnp.bfloat16
    comps = tall_ref.shape[0]
    rows = tall_ref.shape[1]
    width = fetched_ref.shape[0]
    tiles = width // rows
    fetched = fetched_ref[...]
    resampled = jnp.dot(fetched, interp_ref[...], preferred_element_type=single).astype(bfloat)
    model = jnp.zeros((width, rows), single)
    for q in range(comps):
        blurred = jnp.dot(resampled, tall_t_ref[q], preferred_element_type=single).astype(bfloat)
        parts = []
        for i in range(tiles):
            acc = jnp.dot(main_ref[q], blurred[i * rows:(i + 1) * rows], preferred_element_type=single)
            if i > 0:
                acc = acc + jnp.dot(prev_ref[q], blurred[(i - 1) * rows:i * rows], preferred_element_type=single)
            if i < tiles - 1:
                acc = acc + jnp.dot(next_ref[q], blurred[(i + 1) * rows:(i + 2) * rows], preferred_element_type=single)
            parts.append(acc)
        component = jnp.concatenate(parts, axis=0)
        comp_ref[q] = component
        model = model + amp_ref[q:q + 1, :] * component
    weighted = weight_ref[...] * (model - observed_ref[...].astype(single))
    residual = weighted.astype(bfloat)
    lane = lax.broadcasted_iota(jnp.int32, (1, rows), 1)
    terms = jnp.zeros((1, rows), single)
    adjoint = jnp.zeros((width, rows), single)
    for q in range(comps):
        amp_sum = jnp.sum(comp_ref[q] * weighted, keepdims=True)
        terms = terms + jnp.where(lane == q, amp_sum, 0.0)
        parts = []
        for i in range(tiles):
            acc = jnp.dot(main_t_ref[q], residual[i * rows:(i + 1) * rows], preferred_element_type=single)
            if i < tiles - 1:
                acc = acc + jnp.dot(prev_t_ref[q], residual[(i + 1) * rows:(i + 2) * rows], preferred_element_type=single)
            if i > 0:
                acc = acc + jnp.dot(next_t_ref[q], residual[(i - 1) * rows:i * rows], preferred_element_type=single)
            parts.append(acc.astype(bfloat))
        back_wide = jnp.concatenate(parts, axis=0)
        adjoint = adjoint + amp_ref[q:q + 1, :] * jnp.dot(back_wide, tall_ref[q], preferred_element_type=single)
    slope = jnp.dot(fetched, slope_ref[...], preferred_element_type=single)
    shift_sum = jnp.sum(adjoint * slope, keepdims=True)
    terms = terms + jnp.where(lane == comps, shift_sum, 0.0)
    terms_ref[...] = jnp.broadcast_to(terms, terms_ref.shape)
    grad_ref[...] = jnp.dot(adjoint.astype(bfloat), interp_t_ref[...], preferred_element_type=single).astype(bfloat)


def run_block(fetched, observed, weight, amp_rows, interp, slope_map, tall, main, prev, nxt):
    width, rows = fetched.shape
    comps = tall.shape[0]
    swap = lambda a: jnp.swapaxes(a, -1, -2)
    vm = pl.BlockSpec(memory_space=pltpu.VMEM)
    grad, terms = pl.pallas_call(
        block_kernel,
        out_shape=(
            jax.ShapeDtypeStruct((width, rows), jnp.bfloat16),
            jax.ShapeDtypeStruct((8, rows), jnp.float32),
        ),
        in_specs=[vm] * 15,
        out_specs=(vm, vm),
        scratch_shapes=[pltpu.VMEM((comps, width, rows), jnp.float32)],
    )(fetched, observed, weight, amp_rows, interp, swap(interp), slope_map, swap(tall), tall,
      main, prev, nxt, swap(main), swap(prev), swap(nxt))
    return grad, terms[0]


def body(
    sky_model,
    observed,
    row_weight,
    foot_owner,
    foot_local,
    row_offset,
    exposure_of,
    amplitude,
    subpixel_shift,
    column_profile,
    row_profile,
):
    tile_count = lax.axis_size("tile")
    seg_count = sky_model.shape[1]
    block_rows = sky_model.shape[2]
    block_count = observed.shape[1]
    width = observed.shape[2]
    capacity = 2 * block_count * width // tile_count
    expo_count = amplitude.shape[1]
    comp_count = amplitude.shape[0]
    tile_blocks = width // block_rows
    requests = block_count * width
    pixels = width * block_rows
    highest = lax.Precision.HIGHEST
    bfloat = jnp.bfloat16
    single = jnp.float32
    request_owner = foot_owner.reshape(requests)
    request_local = foot_local.reshape(requests)
    owner_hits = (
        request_owner.reshape(block_count, width)[:, :, None]
        == jnp.arange(tile_count, dtype=jnp.int32)[None, None, :]
    )
    owner_onehot = owner_hits.astype(bfloat)
    within = jnp.einsum(
        "uy,byt->but", strict_lower(width), owner_onehot, preferred_element_type=single
    )
    block_totals = jnp.sum(owner_onehot.astype(single), axis=1)
    before = jnp.dot(strict_lower(block_count).astype(single), block_totals, precision=highest)
    rank_table = jnp.where(owner_hits, within + before[:, None, :], jnp.zeros((), single))
    owner_rank = jnp.sum(rank_table, axis=2).astype(jnp.int32).reshape(requests)
    slot_index = request_owner * capacity + owner_rank
    slot_iota = jnp.arange(tile_count * capacity, dtype=jnp.int32)
    slot_onehot_t = (slot_iota[:, None] == slot_index[None, :]).astype(bfloat)
    request_code = request_local + 1
    request_parts = jnp.stack([request_code // 32, request_code % 32], axis=1).astype(bfloat)
    request_sums = jnp.dot(slot_onehot_t, request_parts, preferred_element_type=single)
    request_ids = (
        request_sums[:, 0].astype(jnp.int32) * 32 + request_sums[:, 1].astype(jnp.int32)
    ).reshape(tile_count, capacity)
    block_offset = row_offset.reshape(block_count)
    block_exposure = exposure_of.reshape(block_count)
    served_ids = lax.all_to_all(request_ids, "tile", split_axis=0, concat_axis=0, tiled=True)
    served_valid = served_ids > 0
    served_where = jnp.maximum(served_ids - 1, 0)
    local_sky = sky_model[0]
    served_flat = served_ids.reshape(tile_count * capacity) - 1
    seg_iota = jnp.arange(seg_count, dtype=jnp.int32)
    serve_onehot = (served_flat[:, None] == seg_iota[None, :]).astype(bfloat)
    picked_rows = jnp.dot(serve_onehot, local_sky, preferred_element_type=single).astype(bfloat)
    served_rows = picked_rows.reshape(tile_count, capacity, block_rows)
    returned = lax.all_to_all(served_rows, "tile", split_axis=0, concat_axis=0, tiled=True)
    slot_onehot = (slot_index[:, None] == slot_iota[None, :]).astype(bfloat)
    fetched = (
        jnp.dot(
            slot_onehot,
            returned.reshape(tile_count * capacity, block_rows),
            preferred_element_type=single,
        )
        .astype(bfloat)
        .reshape(block_count, width, block_rows)
    )
    expo_onehot = (
        block_exposure[:, None] == jnp.arange(expo_count, dtype=jnp.int32)[None, :]
    ).astype(single)
    block_amp = jnp.dot(expo_onehot, amplitude.T, precision=highest)
    block_frac = jnp.dot(expo_onehot, subpixel_shift, precision=highest)
    block_wide = jnp.einsum("be,eqt->bqt", expo_onehot, column_profile, precision=highest)
    block_tall = jnp.einsum("be,eqt->bqt", expo_onehot, row_profile, precision=highest)
    j_index = jnp.arange(block_rows, dtype=jnp.int32)[None, :, None]
    v_index = jnp.arange(block_rows, dtype=jnp.int32)[None, None, :]
    offsets = block_offset[:, None, None]
    lower_hit = j_index == v_index + offsets
    upper_hit = j_index == v_index + offsets + 1
    zero_b = jnp.zeros((), bfloat)
    weight_low = (1.0 - block_frac).astype(bfloat)[:, None, None]
    weight_high = block_frac.astype(bfloat)[:, None, None]
    interp = jnp.where(lower_hit, weight_low, zero_b) + jnp.where(upper_hit, weight_high, zero_b)
    slope_map = upper_hit.astype(bfloat) - lower_hit.astype(bfloat)
    tall_kernel = band_lookup(block_tall.astype(bfloat), 0, block_rows)
    wide_profile_b = block_wide.astype(bfloat)
    wide_main = band_lookup(wide_profile_b, 0, block_rows)
    wide_prev = band_lookup(wide_profile_b, -block_rows, block_rows)
    wide_next = band_lookup(wide_profile_b, block_rows, block_rows)
    weight_rows = row_weight.reshape(block_count, block_rows)
    observed_blocks = observed[0]
    block_results = [
        run_block(
            fetched[b],
            observed_blocks[b],
            weight_rows[b][None, :],
            jnp.broadcast_to(block_amp[b][:, None], (comp_count, block_rows)),
            interp[b],
            slope_map[b],
            tall_kernel[b],
            wide_main[b],
            wide_prev[b],
            wide_next[b],
        )
        for b in range(block_count)
    ]
    segment_grad = jnp.stack([grad for grad, _ in block_results])
    block_sums = jnp.stack([terms for _, terms in block_results])
    block_terms = block_sums[:, : comp_count + 1] / pixels
    term_count = comp_count + 1
    terms_high = lax.reduce_precision(block_terms, exponent_bits=8, mantissa_bits=7)
    terms_low = block_terms - terms_high
    term_row = jnp.concatenate(
        [
            terms_high.astype(bfloat),
            terms_low.astype(bfloat),
            block_exposure.astype(bfloat)[:, None],
        ],
        axis=1,
    ).reshape(block_count * (2 * term_count + 1))
    term_row = jnp.pad(term_row, (0, block_rows - term_row.shape[0]))
    send_grad = (
        jnp.dot(
            slot_onehot_t,
            segment_grad.reshape(requests, block_rows).astype(bfloat),
            preferred_element_type=single,
        )
        .astype(bfloat)
        .reshape(tile_count, capacity, block_rows)
    )
    send_all = jnp.concatenate(
        [
            send_grad.astype(bfloat),
            jnp.broadcast_to(term_row[None, None, :], (tile_count, 1, block_rows)),
        ],
        axis=1,
    )
    received = lax.all_to_all(send_all, "tile", split_axis=0, concat_axis=0, tiled=True)
    segment_rows = received[:, :capacity]
    peer_rows = received[:, capacity, : block_count * (2 * term_count + 1)].astype(single)
    peer_rows = peer_rows.reshape(tile_count * block_count, 2 * term_count + 1)
    peer_terms = peer_rows[:, :term_count] + peer_rows[:, term_count : 2 * term_count]
    peer_onehot = (
        peer_rows[:, 2 * term_count][:, None] == jnp.arange(expo_count, dtype=single)[None, :]
    ).astype(single)
    partial_params = jnp.dot(peer_terms.T, peer_onehot, precision=highest)
    flat_rows = segment_rows.reshape(tile_count * capacity, block_rows)
    serve_onehot_t = (seg_iota[:, None] == served_flat[None, :]).astype(bfloat)
    grad_local = jnp.dot(serve_onehot_t, flat_rows, preferred_element_type=single)
    grad_params = lax.psum(partial_params, "band")
    return (grad_local[None], grad_params)


def solution(mesh):
    placed = (
        P("band", "tile", None),
        P("band", "tile", None, None),
        P("band", "tile", None),
        P("band", "tile", None, None),
        P("band", "tile", None),
        P("band", "tile"),
        P("band", "tile"),
        P(),
        P(),
        P(),
        P(),
    )
    return jax.shard_map(
        body, mesh=mesh, in_specs=placed, out_specs=(P("band", "tile", None), P()), check_vma=False
    )
```

```python
import functools
import jax
import jax.numpy as jnp
from jax import lax
from jax.sharding import PartitionSpec as P
from jax.experimental import pallas as pl
from jax.experimental.pallas import tpu as pltpu


def band_lookup(profile, lag_shift, size):
    taps = profile.shape[-1]
    out_index = jnp.arange(size, dtype=jnp.int32)[:, None]
    in_index = jnp.arange(size, dtype=jnp.int32)[None, :]
    lag = in_index - out_index + taps // 2 + lag_shift
    tap_mask = (lag[:, :, None] == jnp.arange(taps, dtype=jnp.int32)[None, None, :]).astype(
        jnp.bfloat16
    )
    return jnp.einsum(
        "vwt,bqt->bqvw", tap_mask, profile, preferred_element_type=jnp.float32
    ).astype(jnp.bfloat16)


def from_previous(values):
    blank = jnp.zeros_like(values[:, :, :1])
    return jnp.concatenate([blank, values[:, :, :-1]], axis=2)


def from_next(values):
    blank = jnp.zeros_like(values[:, :, :1])
    return jnp.concatenate([values[:, :, 1:], blank], axis=2)


def strict_lower(size):
    above = jnp.arange(size, dtype=jnp.int32)[:, None]
    below = jnp.arange(size, dtype=jnp.int32)[None, :]
    return (below < above).astype(jnp.bfloat16)


def block_kernel(
    amp_ref, slot_col_ref, slot_row_ref, returned_ref, observed_ref, weight_ref, interp_ref,
    interp_t_ref, slope_ref, tall_t_ref, tall_ref, main_ref, prev_ref, next_ref, main_t_ref,
    prev_t_ref, next_t_ref, send_ref, terms_ref, comp_ref,
):
    single = jnp.float32
    bfloat = jnp.bfloat16
    comps = tall_ref.shape[0]
    rows = tall_ref.shape[1]
    width = observed_ref.shape[0]
    slots = returned_ref.shape[0]
    tiles = width // rows
    pick = (
        slot_col_ref[...] == lax.broadcasted_iota(jnp.int32, (width, slots), 1)
    ).astype(bfloat)
    fetched = jnp.dot(pick, returned_ref[...], preferred_element_type=single).astype(bfloat)
    resampled = jnp.dot(fetched, interp_ref[...], preferred_element_type=single).astype(bfloat)
    model = jnp.zeros((width, rows), single)
    for q in range(comps):
        blurred = jnp.dot(resampled, tall_t_ref[q], preferred_element_type=single).astype(bfloat)
        parts = []
        for i in range(tiles):
            acc = jnp.dot(main_ref[q], blurred[i * rows:(i + 1) * rows], preferred_element_type=single)
            if i > 0:
                acc = acc + jnp.dot(prev_ref[q], blurred[(i - 1) * rows:i * rows], preferred_element_type=single)
            if i < tiles - 1:
                acc = acc + jnp.dot(next_ref[q], blurred[(i + 1) * rows:(i + 2) * rows], preferred_element_type=single)
            parts.append(acc)
        component = jnp.concatenate(parts, axis=0)
        comp_ref[q] = component
        model = model + amp_ref[q] * component
    weighted = weight_ref[...] * (model - observed_ref[...].astype(single))
    residual = weighted.astype(bfloat)
    lane = lax.broadcasted_iota(jnp.int32, (1, rows), 1)
    terms = jnp.zeros((1, rows), single)
    adjoint = jnp.zeros((width, rows), single)
    for q in range(comps):
        amp_sum = jnp.sum(comp_ref[q] * weighted, keepdims=True)
        terms = terms + jnp.where(lane == q, amp_sum, 0.0)
        parts = []
        for i in range(tiles):
            acc = jnp.dot(main_t_ref[q], residual[i * rows:(i + 1) * rows], preferred_element_type=single)
            if i < tiles - 1:
                acc = acc + jnp.dot(prev_t_ref[q], residual[(i + 1) * rows:(i + 2) * rows], preferred_element_type=single)
            if i > 0:
                acc = acc + jnp.dot(next_t_ref[q], residual[(i - 1) * rows:i * rows], preferred_element_type=single)
            parts.append(acc.astype(bfloat))
        back_wide = jnp.concatenate(parts, axis=0)
        adjoint = adjoint + amp_ref[q] * jnp.dot(back_wide, tall_ref[q], preferred_element_type=single)
    slope = jnp.dot(fetched, slope_ref[...], preferred_element_type=single)
    shift_sum = jnp.sum(adjoint * slope, keepdims=True)
    terms = terms + jnp.where(lane == comps, shift_sum, 0.0)
    terms_ref[...] = jnp.broadcast_to(terms, terms_ref.shape)
    grad = jnp.dot(adjoint.astype(bfloat), interp_t_ref[...], preferred_element_type=single).astype(bfloat)
    place = (
        lax.broadcasted_iota(jnp.int32, (slots, width), 0) == slot_row_ref[...]
    ).astype(bfloat)
    send_ref[...] = jnp.dot(place, grad, preferred_element_type=single).astype(bfloat)


def run_block(amps, slot_index, returned, observed, weight, interp, slope_map, tall, main, prev, nxt):
    width, rows = observed.shape
    slots = returned.shape[0]
    comps = tall.shape[0]
    swap = lambda a: jnp.swapaxes(a, -1, -2)
    vm = pl.BlockSpec(memory_space=pltpu.VMEM)
    sm = pl.BlockSpec(memory_space=pltpu.SMEM)
    send, terms = pl.pallas_call(
        block_kernel,
        out_shape=(
            jax.ShapeDtypeStruct((slots, rows), jnp.bfloat16),
            jax.ShapeDtypeStruct((8, rows), jnp.float32),
        ),
        in_specs=[sm] + [vm] * 16,
        out_specs=(vm, vm),
        scratch_shapes=[pltpu.VMEM((comps, width, rows), jnp.float32)],
    )(amps, slot_index[:, None], slot_index[None, :], returned, observed, weight, interp,
      swap(interp), slope_map, swap(tall), tall, main, prev, nxt, swap(main), swap(prev), swap(nxt))
    return send, terms[0]


def body(
    sky_model,
    observed,
    row_weight,
    foot_owner,
    foot_local,
    row_offset,
    exposure_of,
    amplitude,
    subpixel_shift,
    column_profile,
    row_profile,
):
    tile_count = lax.axis_size("tile")
    seg_count = sky_model.shape[1]
    block_rows = sky_model.shape[2]
    block_count = observed.shape[1]
    width = observed.shape[2]
    capacity = 2 * block_count * width // tile_count
    expo_count = amplitude.shape[1]
    comp_count = amplitude.shape[0]
    tile_blocks = width // block_rows
    requests = block_count * width
    pixels = width * block_rows
    highest = lax.Precision.HIGHEST
    bfloat = jnp.bfloat16
    single = jnp.float32
    request_owner = foot_owner.reshape(requests)
    request_local = foot_local.reshape(requests)
    owner_hits = (
        request_owner.reshape(block_count, width)[:, :, None]
        == jnp.arange(tile_count, dtype=jnp.int32)[None, None, :]
    )
    owner_onehot = owner_hits.astype(bfloat)
    within = jnp.einsum(
        "uy,byt->but", strict_lower(width), owner_onehot, preferred_element_type=single
    )
    block_totals = jnp.sum(owner_onehot.astype(single), axis=1)
    before = jnp.dot(strict_lower(block_count).astype(single), block_totals, precision=highest)
    rank_table = jnp.where(owner_hits, within + before[:, None, :], jnp.zeros((), single))
    owner_rank = jnp.sum(rank_table, axis=2).astype(jnp.int32).reshape(requests)
    slot_index = request_owner * capacity + owner_rank
    slot_iota = jnp.arange(tile_count * capacity, dtype=jnp.int32)
    slot_onehot_t = (slot_iota[:, None] == slot_index[None, :]).astype(bfloat)
    request_code = request_local + 1
    request_parts = jnp.stack([request_code // 32, request_code % 32], axis=1).astype(bfloat)
    request_sums = jnp.dot(slot_onehot_t, request_parts, preferred_element_type=single)
    request_ids = (
        request_sums[:, 0].astype(jnp.int32) * 32 + request_sums[:, 1].astype(jnp.int32)
    ).reshape(tile_count, capacity)
    block_offset = row_offset.reshape(block_count)
    block_exposure = exposure_of.reshape(block_count)
    served_ids = lax.all_to_all(request_ids, "tile", split_axis=0, concat_axis=0, tiled=True)
    served_valid = served_ids > 0
    served_where = jnp.maximum(served_ids - 1, 0)
    local_sky = sky_model[0]
    served_flat = served_ids.reshape(tile_count * capacity) - 1
    seg_iota = jnp.arange(seg_count, dtype=jnp.int32)
    serve_onehot = (served_flat[:, None] == seg_iota[None, :]).astype(bfloat)
    picked_rows = jnp.dot(serve_onehot, local_sky, preferred_element_type=single).astype(bfloat)
    served_rows = picked_rows.reshape(tile_count, capacity, block_rows)
    returned = lax.all_to_all(served_rows, "tile", split_axis=0, concat_axis=0, tiled=True)
    expo_onehot = (
        block_exposure[:, None] == jnp.arange(expo_count, dtype=jnp.int32)[None, :]
    ).astype(single)
    block_amp = jnp.dot(expo_onehot, amplitude.T, precision=highest)
    block_frac = jnp.dot(expo_onehot, subpixel_shift, precision=highest)
    block_wide = jnp.einsum("be,eqt->bqt", expo_onehot, column_profile, precision=highest)
    block_tall = jnp.einsum("be,eqt->bqt", expo_onehot, row_profile, precision=highest)
    j_index = jnp.arange(block_rows, dtype=jnp.int32)[None, :, None]
    v_index = jnp.arange(block_rows, dtype=jnp.int32)[None, None, :]
    offsets = block_offset[:, None, None]
    lower_hit = j_index == v_index + offsets
    upper_hit = j_index == v_index + offsets + 1
    zero_b = jnp.zeros((), bfloat)
    weight_low = (1.0 - block_frac).astype(bfloat)[:, None, None]
    weight_high = block_frac.astype(bfloat)[:, None, None]
    interp = jnp.where(lower_hit, weight_low, zero_b) + jnp.where(upper_hit, weight_high, zero_b)
    slope_map = upper_hit.astype(bfloat) - lower_hit.astype(bfloat)
    tall_kernel = band_lookup(block_tall.astype(bfloat), 0, block_rows)
    wide_profile_b = block_wide.astype(bfloat)
    wide_main = band_lookup(wide_profile_b, 0, block_rows)
    wide_prev = band_lookup(wide_profile_b, -block_rows, block_rows)
    wide_next = band_lookup(wide_profile_b, block_rows, block_rows)
    weight_rows = row_weight.reshape(block_count, block_rows)
    observed_blocks = observed[0]
    returned_rows = returned.reshape(tile_count * capacity, block_rows)
    slot_blocks = slot_index.reshape(block_count, width)
    block_results = [
        run_block(
            block_amp[b],
            slot_blocks[b],
            returned_rows,
            observed_blocks[b],
            weight_rows[b][None, :],
            interp[b],
            slope_map[b],
            tall_kernel[b],
            wide_main[b],
            wide_prev[b],
            wide_next[b],
        )
        for b in range(block_count)
    ]
    send_grad = functools.reduce(jnp.add, [send for send, _ in block_results]).reshape(
        tile_count, capacity, block_rows
    )
    block_sums = jnp.stack([terms for _, terms in block_results])
    block_terms = block_sums[:, : comp_count + 1] / pixels
    term_count = comp_count + 1
    terms_high = lax.reduce_precision(block_terms, exponent_bits=8, mantissa_bits=7)
    terms_low = block_terms - terms_high
    term_row = jnp.concatenate(
        [
            terms_high.astype(bfloat),
            terms_low.astype(bfloat),
            block_exposure.astype(bfloat)[:, None],
        ],
        axis=1,
    ).reshape(block_count * (2 * term_count + 1))
    term_row = jnp.pad(term_row, (0, block_rows - term_row.shape[0]))
    send_all = jnp.concatenate(
        [
            send_grad.astype(bfloat),
            jnp.broadcast_to(term_row[None, None, :], (tile_count, 1, block_rows)),
        ],
        axis=1,
    )
    received = lax.all_to_all(send_all, "tile", split_axis=0, concat_axis=0, tiled=True)
    segment_rows = received[:, :capacity]
    peer_rows = received[:, capacity, : block_count * (2 * term_count + 1)].astype(single)
    peer_rows = peer_rows.reshape(tile_count * block_count, 2 * term_count + 1)
    peer_terms = peer_rows[:, :term_count] + peer_rows[:, term_count : 2 * term_count]
    peer_onehot = (
        peer_rows[:, 2 * term_count][:, None] == jnp.arange(expo_count, dtype=single)[None, :]
    ).astype(single)
    partial_params = jnp.dot(peer_terms.T, peer_onehot, precision=highest)
    flat_rows = segment_rows.reshape(tile_count * capacity, block_rows)
    serve_onehot_t = (seg_iota[:, None] == served_flat[None, :]).astype(bfloat)
    grad_local = jnp.dot(serve_onehot_t, flat_rows, preferred_element_type=single)
    grad_params = lax.psum(partial_params, "band")
    return (grad_local[None], grad_params)


def solution(mesh):
    placed = (
        P("band", "tile", None),
        P("band", "tile", None, None),
        P("band", "tile", None),
        P("band", "tile", None, None),
        P("band", "tile", None),
        P("band", "tile"),
        P("band", "tile"),
        P(),
        P(),
        P(),
        P(),
    )
    return jax.shard_map(
        body, mesh=mesh, in_specs=placed, out_specs=(P("band", "tile", None), P()), check_vma=False
    )
```

```python
import jax
import jax.numpy as jnp
from jax import lax
from jax.sharding import PartitionSpec as P
from jax.experimental import pallas as pl
from jax.experimental.pallas import tpu as pltpu


def band_lookup(profile, lag_shift, size):
    taps = profile.shape[-1]
    out_index = jnp.arange(size, dtype=jnp.int32)[:, None]
    in_index = jnp.arange(size, dtype=jnp.int32)[None, :]
    lag = in_index - out_index + taps // 2 + lag_shift
    tap_mask = (lag[:, :, None] == jnp.arange(taps, dtype=jnp.int32)[None, None, :]).astype(
        jnp.bfloat16
    )
    return jnp.einsum(
        "vwt,bqt->bqvw", tap_mask, profile, preferred_element_type=jnp.float32
    ).astype(jnp.bfloat16)


def from_previous(values):
    blank = jnp.zeros_like(values[:, :, :1])
    return jnp.concatenate([blank, values[:, :, :-1]], axis=2)


def from_next(values):
    blank = jnp.zeros_like(values[:, :, :1])
    return jnp.concatenate([values[:, :, 1:], blank], axis=2)


def strict_lower(size):
    above = jnp.arange(size, dtype=jnp.int32)[:, None]
    below = jnp.arange(size, dtype=jnp.int32)[None, :]
    return (below < above).astype(jnp.bfloat16)


LOW_LANE = 32
EXPO_LANE = 64


def block_kernel(
    amp_ref, expo_ref, slot_col_ref, slot_row_ref, returned_ref, observed_ref, weight_ref, interp_ref,
    interp_t_ref, slope_ref, tall_t_ref, tall_ref, main_ref, prev_ref, next_ref, main_t_ref,
    prev_t_ref, next_t_ref, send_ref, comp_ref,
):
    single = jnp.float32
    bfloat = jnp.bfloat16
    comps = tall_ref.shape[0]
    rows = tall_ref.shape[1]
    width = observed_ref.shape[0]
    slots = returned_ref.shape[0]
    tiles = width // rows
    pick = (
        slot_col_ref[...] == lax.broadcasted_iota(jnp.int32, (width, slots), 1)
    ).astype(bfloat)
    fetched = jnp.dot(pick, returned_ref[...], preferred_element_type=single).astype(bfloat)
    resampled = jnp.dot(fetched, interp_ref[...], preferred_element_type=single).astype(bfloat)
    model = jnp.zeros((width, rows), single)
    for q in range(comps):
        blurred = jnp.dot(resampled, tall_t_ref[q], preferred_element_type=single).astype(bfloat)
        parts = []
        for i in range(tiles):
            acc = jnp.dot(main_ref[q], blurred[i * rows:(i + 1) * rows], preferred_element_type=single)
            if i > 0:
                acc = acc + jnp.dot(prev_ref[q], blurred[(i - 1) * rows:i * rows], preferred_element_type=single)
            if i < tiles - 1:
                acc = acc + jnp.dot(next_ref[q], blurred[(i + 1) * rows:(i + 2) * rows], preferred_element_type=single)
            parts.append(acc)
        component = jnp.concatenate(parts, axis=0)
        comp_ref[q] = component
        model = model + amp_ref[q] * component
    weighted = weight_ref[...] * (model - observed_ref[...].astype(single))
    residual = weighted.astype(bfloat)
    lane = lax.broadcasted_iota(jnp.int32, (1, rows), 1)
    scale = 1.0 / (width * rows)

    def put(terms, total, k):
        total = total * scale
        high = total.astype(bfloat).astype(single)
        low = total - high
        terms = terms + jnp.where(lane == k, high, 0.0)
        return terms + jnp.where(lane == LOW_LANE + k, low, 0.0)

    terms = jnp.zeros((1, rows), single)
    adjoint = jnp.zeros((width, rows), single)
    for q in range(comps):
        amp_sum = jnp.sum(comp_ref[q] * weighted, keepdims=True)
        terms = put(terms, amp_sum, q)
        parts = []
        for i in range(tiles):
            acc = jnp.dot(main_t_ref[q], residual[i * rows:(i + 1) * rows], preferred_element_type=single)
            if i < tiles - 1:
                acc = acc + jnp.dot(prev_t_ref[q], residual[(i + 1) * rows:(i + 2) * rows], preferred_element_type=single)
            if i > 0:
                acc = acc + jnp.dot(next_t_ref[q], residual[(i - 1) * rows:i * rows], preferred_element_type=single)
            parts.append(acc.astype(bfloat))
        back_wide = jnp.concatenate(parts, axis=0)
        adjoint = adjoint + amp_ref[q] * jnp.dot(back_wide, tall_ref[q], preferred_element_type=single)
    slope = jnp.dot(fetched, slope_ref[...], preferred_element_type=single)
    shift_sum = jnp.sum(adjoint * slope, keepdims=True)
    terms = put(terms, shift_sum, comps)
    terms = terms + jnp.where(lane == EXPO_LANE, expo_ref[0].astype(single), 0.0)
    term_row = terms.astype(bfloat)
    grad = jnp.dot(adjoint.astype(bfloat), interp_t_ref[...], preferred_element_type=single).astype(bfloat)
    place = (
        lax.broadcasted_iota(jnp.int32, (slots, width), 0) == slot_row_ref[...]
    ).astype(bfloat)
    send = jnp.dot(place, grad, preferred_element_type=single).astype(bfloat)
    peers = send_ref.shape[0]
    capacity = send_ref.shape[1] - 1
    for p in range(peers):
        send_ref[p, 0:capacity, :] = send[p * capacity:(p + 1) * capacity]
        send_ref[p, capacity:capacity + 1, :] = term_row


def run_block(amps, expo, slot_index, returned, observed, weight, interp, slope_map, tall, main, prev, nxt, peers):
    width, rows = observed.shape
    slots = returned.shape[0]
    comps = tall.shape[0]
    swap = lambda a: jnp.swapaxes(a, -1, -2)
    vm = pl.BlockSpec(memory_space=pltpu.VMEM)
    sm = pl.BlockSpec(memory_space=pltpu.SMEM)
    return pl.pallas_call(
        block_kernel,
        out_shape=jax.ShapeDtypeStruct((peers, slots // peers + 1, rows), jnp.bfloat16),
        in_specs=[sm, sm] + [vm] * 16,
        out_specs=vm,
        scratch_shapes=[pltpu.VMEM((comps, width, rows), jnp.float32)],
    )(amps, expo, slot_index[:, None], slot_index[None, :], returned, observed, weight, interp,
      swap(interp), slope_map, swap(tall), tall, main, prev, nxt, swap(main), swap(prev), swap(nxt))


def body(
    sky_model,
    observed,
    row_weight,
    foot_owner,
    foot_local,
    row_offset,
    exposure_of,
    amplitude,
    subpixel_shift,
    column_profile,
    row_profile,
):
    tile_count = lax.axis_size("tile")
    seg_count = sky_model.shape[1]
    block_rows = sky_model.shape[2]
    block_count = observed.shape[1]
    width = observed.shape[2]
    capacity = 2 * block_count * width // tile_count
    expo_count = amplitude.shape[1]
    comp_count = amplitude.shape[0]
    tile_blocks = width // block_rows
    requests = block_count * width
    pixels = width * block_rows
    highest = lax.Precision.HIGHEST
    bfloat = jnp.bfloat16
    single = jnp.float32
    request_owner = foot_owner.reshape(requests)
    request_local = foot_local.reshape(requests)
    owner_hits = (
        request_owner.reshape(block_count, width)[:, :, None]
        == jnp.arange(tile_count, dtype=jnp.int32)[None, None, :]
    )
    owner_onehot = owner_hits.astype(bfloat)
    within = jnp.einsum(
        "uy,byt->but", strict_lower(width), owner_onehot, preferred_element_type=single
    )
    block_totals = jnp.sum(owner_onehot.astype(single), axis=1)
    before = jnp.dot(strict_lower(block_count).astype(single), block_totals, precision=highest)
    rank_table = jnp.where(owner_hits, within + before[:, None, :], jnp.zeros((), single))
    owner_rank = jnp.sum(rank_table, axis=2).astype(jnp.int32).reshape(requests)
    slot_index = request_owner * capacity + owner_rank
    slot_iota = jnp.arange(tile_count * capacity, dtype=jnp.int32)
    slot_onehot_t = (slot_iota[:, None] == slot_index[None, :]).astype(bfloat)
    request_code = request_local + 1
    request_parts = jnp.stack([request_code // 32, request_code % 32], axis=1).astype(bfloat)
    request_sums = jnp.dot(slot_onehot_t, request_parts, preferred_element_type=single)
    request_ids = (
        request_sums[:, 0].astype(jnp.int32) * 32 + request_sums[:, 1].astype(jnp.int32)
    ).reshape(tile_count, capacity)
    block_offset = row_offset.reshape(block_count)
    block_exposure = exposure_of.reshape(block_count)
    served_ids = lax.all_to_all(request_ids, "tile", split_axis=0, concat_axis=0, tiled=True)
    served_valid = served_ids > 0
    served_where = jnp.maximum(served_ids - 1, 0)
    local_sky = sky_model[0]
    served_flat = served_ids.reshape(tile_count * capacity) - 1
    seg_iota = jnp.arange(seg_count, dtype=jnp.int32)
    serve_onehot = (served_flat[:, None] == seg_iota[None, :]).astype(bfloat)
    picked_rows = jnp.dot(serve_onehot, local_sky, preferred_element_type=single).astype(bfloat)
    served_rows = picked_rows.reshape(tile_count, capacity, block_rows)
    returned = lax.all_to_all(served_rows, "tile", split_axis=0, concat_axis=0, tiled=True)
    expo_onehot = (
        block_exposure[:, None] == jnp.arange(expo_count, dtype=jnp.int32)[None, :]
    ).astype(single)
    block_amp = jnp.dot(expo_onehot, amplitude.T, precision=highest)
    block_frac = jnp.dot(expo_onehot, subpixel_shift, precision=highest)
    block_wide = jnp.einsum("be,eqt->bqt", expo_onehot, column_profile, precision=highest)
    block_tall = jnp.einsum("be,eqt->bqt", expo_onehot, row_profile, precision=highest)
    j_index = jnp.arange(block_rows, dtype=jnp.int32)[None, :, None]
    v_index = jnp.arange(block_rows, dtype=jnp.int32)[None, None, :]
    offsets = block_offset[:, None, None]
    lower_hit = j_index == v_index + offsets
    upper_hit = j_index == v_index + offsets + 1
    zero_b = jnp.zeros((), bfloat)
    weight_low = (1.0 - block_frac).astype(bfloat)[:, None, None]
    weight_high = block_frac.astype(bfloat)[:, None, None]
    interp = jnp.where(lower_hit, weight_low, zero_b) + jnp.where(upper_hit, weight_high, zero_b)
    slope_map = upper_hit.astype(bfloat) - lower_hit.astype(bfloat)
    tall_kernel = band_lookup(block_tall.astype(bfloat), 0, block_rows)
    wide_profile_b = block_wide.astype(bfloat)
    wide_main = band_lookup(wide_profile_b, 0, block_rows)
    wide_prev = band_lookup(wide_profile_b, -block_rows, block_rows)
    wide_next = band_lookup(wide_profile_b, block_rows, block_rows)
    weight_rows = row_weight.reshape(block_count, block_rows)
    observed_blocks = observed[0]
    returned_rows = returned.reshape(tile_count * capacity, block_rows)
    assert block_count == 1
    term_count = comp_count + 1
    send_all = run_block(
        block_amp[0],
        block_exposure,
        slot_index,
        returned_rows,
        observed_blocks[0],
        weight_rows[0][None, :],
        interp[0],
        slope_map[0],
        tall_kernel[0],
        wide_main[0],
        wide_prev[0],
        wide_next[0],
        tile_count,
    )
    received = lax.all_to_all(send_all, "tile", split_axis=0, concat_axis=0, tiled=True)
    segment_rows = received[:, :capacity]
    peer_rows = received[:, capacity, :].astype(single)
    peer_terms = peer_rows[:, :term_count] + peer_rows[:, LOW_LANE : LOW_LANE + term_count]
    peer_onehot = (
        peer_rows[:, EXPO_LANE][:, None] == jnp.arange(expo_count, dtype=single)[None, :]
    ).astype(single)
    partial_params = jnp.dot(peer_terms.T, peer_onehot, precision=highest)
    flat_rows = segment_rows.reshape(tile_count * capacity, block_rows)
    serve_onehot_t = (seg_iota[:, None] == served_flat[None, :]).astype(bfloat)
    grad_local = jnp.dot(serve_onehot_t, flat_rows, preferred_element_type=single)
    grad_params = lax.psum(partial_params, "band")
    return (grad_local[None], grad_params)


def solution(mesh):
    placed = (
        P("band", "tile", None),
        P("band", "tile", None, None),
        P("band", "tile", None),
        P("band", "tile", None, None),
        P("band", "tile", None),
        P("band", "tile"),
        P("band", "tile"),
        P(),
        P(),
        P(),
        P(),
    )
    return jax.shard_map(
        body, mesh=mesh, in_specs=placed, out_specs=(P("band", "tile", None), P()), check_vma=False
    )
```

```python
import jax
import jax.numpy as jnp
from jax import lax
from jax.sharding import PartitionSpec as P
from jax.experimental import pallas as pl
from jax.experimental.pallas import tpu as pltpu


def band_lookup(profile, lag_shift, size):
    taps = profile.shape[-1]
    out_index = jnp.arange(size, dtype=jnp.int32)[:, None]
    in_index = jnp.arange(size, dtype=jnp.int32)[None, :]
    lag = in_index - out_index + taps // 2 + lag_shift
    tap_mask = (lag[:, :, None] == jnp.arange(taps, dtype=jnp.int32)[None, None, :]).astype(
        jnp.bfloat16
    )
    return jnp.einsum(
        "vwt,bqt->bqvw", tap_mask, profile, preferred_element_type=jnp.float32
    ).astype(jnp.bfloat16)


def from_previous(values):
    blank = jnp.zeros_like(values[:, :, :1])
    return jnp.concatenate([blank, values[:, :, :-1]], axis=2)


def from_next(values):
    blank = jnp.zeros_like(values[:, :, :1])
    return jnp.concatenate([values[:, :, 1:], blank], axis=2)


def strict_lower(size):
    above = jnp.arange(size, dtype=jnp.int32)[:, None]
    below = jnp.arange(size, dtype=jnp.int32)[None, :]
    return (below < above).astype(jnp.bfloat16)


LOW_LANE = 32
EXPO_LANE = 64


def block_kernel(
    amp_ref, expo_ref, slot_col_ref, slot_row_ref, returned_ref, observed_ref, weight_ref, interp_ref,
    interp_t_ref, slope_ref, tall_t_ref, tall_ref, main_ref, prev_ref, next_ref, main_t_ref,
    prev_t_ref, next_t_ref, send_ref, comp_ref,
):
    single = jnp.float32
    bfloat = jnp.bfloat16
    comps = tall_ref.shape[0]
    rows = tall_ref.shape[1]
    width = observed_ref.shape[0]
    slots = returned_ref.shape[0]
    tiles = width // rows
    pick = (
        slot_col_ref[...] == lax.broadcasted_iota(jnp.int32, (width, slots), 1)
    ).astype(bfloat)
    fetched = jnp.dot(pick, returned_ref[...], preferred_element_type=single).astype(bfloat)
    resampled = jnp.dot(fetched, interp_ref[...], preferred_element_type=single).astype(bfloat)
    model = jnp.zeros((width, rows), single)
    for q in range(comps):
        blurred = jnp.dot(resampled, tall_t_ref[q], preferred_element_type=single).astype(bfloat)
        parts = []
        for i in range(tiles):
            acc = jnp.dot(main_ref[q], blurred[i * rows:(i + 1) * rows], preferred_element_type=single)
            if i > 0:
                acc = acc + jnp.dot(prev_ref[q], blurred[(i - 1) * rows:i * rows], preferred_element_type=single)
            if i < tiles - 1:
                acc = acc + jnp.dot(next_ref[q], blurred[(i + 1) * rows:(i + 2) * rows], preferred_element_type=single)
            parts.append(acc)
        component = jnp.concatenate(parts, axis=0)
        comp_ref[q] = component
        model = model + amp_ref[q] * component
    weighted = weight_ref[...] * (model - observed_ref[...].astype(single))
    residual = weighted.astype(bfloat)
    lane = lax.broadcasted_iota(jnp.int32, (1, rows), 1)
    scale = 1.0 / (width * rows)

    def put(terms, total, k):
        total = total * scale
        high = total.astype(bfloat).astype(single)
        low = total - high
        terms = terms + jnp.where(lane == k, high, 0.0)
        return terms + jnp.where(lane == LOW_LANE + k, low, 0.0)

    terms = jnp.zeros((1, rows), single)
    adjoint = jnp.zeros((width, rows), single)
    for q in range(comps):
        amp_sum = jnp.sum(comp_ref[q] * weighted, keepdims=True)
        terms = put(terms, amp_sum, q)
        parts = []
        for i in range(tiles):
            acc = jnp.dot(main_t_ref[q], residual[i * rows:(i + 1) * rows], preferred_element_type=single)
            if i < tiles - 1:
                acc = acc + jnp.dot(prev_t_ref[q], residual[(i + 1) * rows:(i + 2) * rows], preferred_element_type=single)
            if i > 0:
                acc = acc + jnp.dot(next_t_ref[q], residual[(i - 1) * rows:i * rows], preferred_element_type=single)
            parts.append(acc.astype(bfloat))
        back_wide = jnp.concatenate(parts, axis=0)
        adjoint = adjoint + amp_ref[q] * jnp.dot(back_wide, tall_ref[q], preferred_element_type=single)
    slope = jnp.dot(fetched, slope_ref[...], preferred_element_type=single)
    shift_sum = jnp.sum(adjoint * slope, keepdims=True)
    terms = put(terms, shift_sum, comps)
    terms = terms + jnp.where(lane == EXPO_LANE, expo_ref[0].astype(single), 0.0)
    term_row = terms.astype(bfloat)
    grad = jnp.dot(adjoint.astype(bfloat), interp_t_ref[...], preferred_element_type=single).astype(bfloat)
    place = (
        lax.broadcasted_iota(jnp.int32, (slots, width), 0) == slot_row_ref[...]
    ).astype(bfloat)
    send = jnp.dot(place, grad, preferred_element_type=single).astype(bfloat)
    peers = send_ref.shape[0]
    capacity = send_ref.shape[1] - 1
    for p in range(peers):
        send_ref[p, 0:capacity, :] = send[p * capacity:(p + 1) * capacity]
        send_ref[p, capacity:capacity + 1, :] = term_row


def run_block(amps, expo, slot_index, returned, observed, weight, interp, slope_map, tall, main, prev, nxt, peers):
    width, rows = observed.shape
    slots = returned.shape[0]
    comps = tall.shape[0]
    swap = lambda a: jnp.swapaxes(a, -1, -2)
    vm = pl.BlockSpec(memory_space=pltpu.VMEM)
    sm = pl.BlockSpec(memory_space=pltpu.SMEM)
    return pl.pallas_call(
        block_kernel,
        out_shape=jax.ShapeDtypeStruct((peers, slots // peers + 1, rows), jnp.bfloat16),
        in_specs=[sm, sm] + [vm] * 16,
        out_specs=vm,
        scratch_shapes=[pltpu.VMEM((comps, width, rows), jnp.float32)],
    )(amps, expo, slot_index[:, None], slot_index[None, :], returned, observed, weight, interp,
      swap(interp), slope_map, swap(tall), tall, main, prev, nxt, swap(main), swap(prev), swap(nxt))


def body(
    sky_model,
    observed,
    row_weight,
    foot_owner,
    foot_local,
    row_offset,
    exposure_of,
    amplitude,
    subpixel_shift,
    column_profile,
    row_profile,
):
    tile_count = lax.axis_size("tile")
    seg_count = sky_model.shape[1]
    block_rows = sky_model.shape[2]
    block_count = observed.shape[1]
    width = observed.shape[2]
    capacity = 2 * block_count * width // tile_count
    expo_count = amplitude.shape[1]
    comp_count = amplitude.shape[0]
    tile_blocks = width // block_rows
    requests = block_count * width
    pixels = width * block_rows
    highest = lax.Precision.HIGHEST
    bfloat = jnp.bfloat16
    single = jnp.float32
    request_owner = foot_owner.reshape(requests)
    request_local = foot_local.reshape(requests)
    owner_hits = (
        request_owner.reshape(block_count, width)[:, :, None]
        == jnp.arange(tile_count, dtype=jnp.int32)[None, None, :]
    )
    owner_onehot = owner_hits.astype(bfloat)
    within = jnp.einsum(
        "uy,byt->but", strict_lower(width), owner_onehot, preferred_element_type=single
    )
    block_totals = jnp.sum(owner_onehot.astype(single), axis=1)
    before = jnp.dot(strict_lower(block_count).astype(single), block_totals, precision=highest)
    rank_table = jnp.where(owner_hits, within + before[:, None, :], jnp.zeros((), single))
    owner_rank = jnp.sum(rank_table, axis=2).astype(jnp.int32).reshape(requests)
    slot_index = request_owner * capacity + owner_rank
    slot_iota = jnp.arange(tile_count * capacity, dtype=jnp.int32)
    slot_onehot_t = (slot_iota[:, None] == slot_index[None, :]).astype(bfloat)
    request_code = request_local + 1
    request_parts = jnp.stack([request_code // 32, request_code % 32], axis=1).astype(bfloat)
    request_sums = jnp.dot(slot_onehot_t, request_parts, preferred_element_type=single)
    request_ids = (
        request_sums[:, 0].astype(jnp.int32) * 32 + request_sums[:, 1].astype(jnp.int32)
    ).reshape(tile_count, capacity)
    block_offset = row_offset.reshape(block_count)
    block_exposure = exposure_of.reshape(block_count)
    served_ids = lax.all_to_all(request_ids, "tile", split_axis=0, concat_axis=0, tiled=True)
    served_valid = served_ids > 0
    served_where = jnp.maximum(served_ids - 1, 0)
    local_sky = sky_model[0]
    served_flat = served_ids.reshape(tile_count * capacity) - 1
    seg_iota = jnp.arange(seg_count, dtype=jnp.int32)
    serve_onehot = (served_flat[:, None] == seg_iota[None, :]).astype(bfloat)
    picked_rows = jnp.dot(serve_onehot, local_sky, preferred_element_type=single).astype(bfloat)
    served_rows = picked_rows.reshape(tile_count, capacity, block_rows)
    returned = lax.all_to_all(served_rows, "tile", split_axis=0, concat_axis=0, tiled=True)
    expo_onehot = (
        block_exposure[:, None] == jnp.arange(expo_count, dtype=jnp.int32)[None, :]
    ).astype(single)
    block_amp = jnp.dot(expo_onehot, amplitude.T, precision=highest)
    block_frac = jnp.dot(expo_onehot, subpixel_shift, precision=highest)
    block_wide = jnp.einsum("be,eqt->bqt", expo_onehot, column_profile, precision=highest)
    block_tall = jnp.einsum("be,eqt->bqt", expo_onehot, row_profile, precision=highest)
    j_index = jnp.arange(block_rows, dtype=jnp.int32)[None, :, None]
    v_index = jnp.arange(block_rows, dtype=jnp.int32)[None, None, :]
    offsets = block_offset[:, None, None]
    lower_hit = j_index == v_index + offsets
    upper_hit = j_index == v_index + offsets + 1
    zero_b = jnp.zeros((), bfloat)
    weight_low = (1.0 - block_frac).astype(bfloat)[:, None, None]
    weight_high = block_frac.astype(bfloat)[:, None, None]
    interp = jnp.where(lower_hit, weight_low, zero_b) + jnp.where(upper_hit, weight_high, zero_b)
    slope_map = upper_hit.astype(bfloat) - lower_hit.astype(bfloat)
    tall_kernel = band_lookup(block_tall.astype(bfloat), 0, block_rows)
    wide_profile_b = block_wide.astype(bfloat)
    wide_main = band_lookup(wide_profile_b, 0, block_rows)
    wide_prev = band_lookup(wide_profile_b, -block_rows, block_rows)
    wide_next = band_lookup(wide_profile_b, block_rows, block_rows)
    weight_rows = row_weight.reshape(block_count, block_rows)
    observed_blocks = observed[0]
    returned_rows = returned.reshape(tile_count * capacity, block_rows)
    assert block_count == 1
    term_count = comp_count + 1
    send_all = run_block(
        block_amp[0],
        block_exposure,
        slot_index,
        returned_rows,
        observed_blocks[0],
        weight_rows[0][None, :],
        interp[0],
        slope_map[0],
        tall_kernel[0],
        wide_main[0],
        wide_prev[0],
        wide_next[0],
        tile_count,
    )
    received = lax.all_to_all(send_all, "tile", split_axis=0, concat_axis=0, tiled=True)
    segment_rows = received[:, :capacity]
    peer_rows = received[:, capacity, :].astype(single)
    peer_terms = peer_rows[:, :term_count] + peer_rows[:, LOW_LANE : LOW_LANE + term_count]
    peer_onehot = (
        peer_rows[:, EXPO_LANE][:, None] == jnp.arange(expo_count, dtype=single)[None, :]
    ).astype(single)
    partial_params = jnp.dot(peer_terms.T, peer_onehot, precision=highest)
    flat_rows = segment_rows.reshape(tile_count * capacity, block_rows)
    serve_onehot_t = (seg_iota[:, None] == served_flat[None, :]).astype(bfloat)
    grad_local = jnp.dot(serve_onehot_t, flat_rows, preferred_element_type=single)
    band_count = lax.axis_size("band")
    band_here = lax.axis_index("band")
    band_parts = [partial_params] + [
        lax.ppermute(
            partial_params,
            "band",
            [(source, (source + step) % band_count) for source in range(band_count)],
        )
        for step in range(1, band_count)
    ]
    band_stack = jnp.stack(band_parts)
    band_order = (band_here - jnp.arange(band_count, dtype=jnp.int32)) % band_count
    band_sorted = jnp.take(band_stack, band_order, axis=0)
    grad_params = band_sorted[0]
    for source in range(1, band_count):
        grad_params = grad_params + band_sorted[source]
    return (grad_local[None], grad_params)


def solution(mesh):
    placed = (
        P("band", "tile", None),
        P("band", "tile", None, None),
        P("band", "tile", None),
        P("band", "tile", None, None),
        P("band", "tile", None),
        P("band", "tile"),
        P("band", "tile"),
        P(),
        P(),
        P(),
        P(),
    )
    return jax.shard_map(
        body, mesh=mesh, in_specs=placed, out_specs=(P("band", "tile", None), P()), check_vma=False
    )
```

```python
import jax
import jax.numpy as jnp
from jax import lax
from jax.sharding import PartitionSpec as P
from jax.experimental import pallas as pl
from jax.experimental.pallas import tpu as pltpu


def band_lookup(profile, lag_shift, size):
    taps = profile.shape[-1]
    out_index = jnp.arange(size, dtype=jnp.int32)[:, None]
    in_index = jnp.arange(size, dtype=jnp.int32)[None, :]
    lag = in_index - out_index + taps // 2 + lag_shift
    tap_mask = (lag[:, :, None] == jnp.arange(taps, dtype=jnp.int32)[None, None, :]).astype(
        jnp.bfloat16
    )
    return jnp.einsum(
        "vwt,bqt->bqvw", tap_mask, profile, preferred_element_type=jnp.float32
    ).astype(jnp.bfloat16)


def from_previous(values):
    blank = jnp.zeros_like(values[:, :, :1])
    return jnp.concatenate([blank, values[:, :, :-1]], axis=2)


def from_next(values):
    blank = jnp.zeros_like(values[:, :, :1])
    return jnp.concatenate([values[:, :, 1:], blank], axis=2)


def strict_lower(size):
    above = jnp.arange(size, dtype=jnp.int32)[:, None]
    below = jnp.arange(size, dtype=jnp.int32)[None, :]
    return (below < above).astype(jnp.bfloat16)


LOW_LANE = 32
EXPO_LANE = 64


def block_kernel(
    amp_ref, expo_ref, slot_col_ref, slot_row_ref, returned_ref, observed_ref, weight_ref, interp_ref,
    interp_t_ref, slope_ref, tall_t_ref, tall_ref, main_ref, prev_ref, next_ref, main_t_ref,
    prev_t_ref, next_t_ref, send_ref, comp_ref,
):
    single = jnp.float32
    bfloat = jnp.bfloat16
    comps = tall_ref.shape[0]
    rows = tall_ref.shape[1]
    width = observed_ref.shape[0]
    slots = returned_ref.shape[0]
    tiles = width // rows
    pick = (
        slot_col_ref[...] == lax.broadcasted_iota(jnp.int32, (width, slots), 1)
    ).astype(bfloat)
    fetched = jnp.dot(pick, returned_ref[...], preferred_element_type=single).astype(bfloat)
    resampled = jnp.dot(fetched, interp_ref[...], preferred_element_type=single).astype(bfloat)
    model = jnp.zeros((width, rows), single)
    for q in range(comps):
        blurred = jnp.dot(resampled, tall_t_ref[q], preferred_element_type=single).astype(bfloat)
        parts = []
        for i in range(tiles):
            acc = jnp.dot(main_ref[q], blurred[i * rows:(i + 1) * rows], preferred_element_type=single)
            if i > 0:
                acc = acc + jnp.dot(prev_ref[q], blurred[(i - 1) * rows:i * rows], preferred_element_type=single)
            if i < tiles - 1:
                acc = acc + jnp.dot(next_ref[q], blurred[(i + 1) * rows:(i + 2) * rows], preferred_element_type=single)
            parts.append(acc)
        component = jnp.concatenate(parts, axis=0)
        comp_ref[q] = component
        model = model + amp_ref[q] * component
    weighted = weight_ref[...] * (model - observed_ref[...].astype(single))
    residual = weighted.astype(bfloat)
    lane = lax.broadcasted_iota(jnp.int32, (1, rows), 1)
    scale = 1.0 / (width * rows)

    def put(terms, total, k):
        total = total * scale
        high = total.astype(bfloat).astype(single)
        low = total - high
        terms = terms + jnp.where(lane == k, high, 0.0)
        return terms + jnp.where(lane == LOW_LANE + k, low, 0.0)

    terms = jnp.zeros((1, rows), single)
    adjoint = jnp.zeros((width, rows), single)
    for q in range(comps):
        amp_sum = jnp.sum(comp_ref[q] * weighted, keepdims=True)
        terms = put(terms, amp_sum, q)
        parts = []
        for i in range(tiles):
            acc = jnp.dot(main_t_ref[q], residual[i * rows:(i + 1) * rows], preferred_element_type=single)
            if i < tiles - 1:
                acc = acc + jnp.dot(prev_t_ref[q], residual[(i + 1) * rows:(i + 2) * rows], preferred_element_type=single)
            if i > 0:
                acc = acc + jnp.dot(next_t_ref[q], residual[(i - 1) * rows:i * rows], preferred_element_type=single)
            parts.append(acc.astype(bfloat))
        back_wide = jnp.concatenate(parts, axis=0)
        adjoint = adjoint + amp_ref[q] * jnp.dot(back_wide, tall_ref[q], preferred_element_type=single)
    slope = jnp.dot(fetched, slope_ref[...], preferred_element_type=single)
    shift_sum = jnp.sum(adjoint * slope, keepdims=True)
    terms = put(terms, shift_sum, comps)
    terms = terms + jnp.where(lane == EXPO_LANE, expo_ref[0].astype(single), 0.0)
    term_row = terms.astype(bfloat)
    grad = jnp.dot(adjoint.astype(bfloat), interp_t_ref[...], preferred_element_type=single).astype(bfloat)
    place = (
        lax.broadcasted_iota(jnp.int32, (slots, width), 0) == slot_row_ref[...]
    ).astype(bfloat)
    send = jnp.dot(place, grad, preferred_element_type=single).astype(bfloat)
    peers = send_ref.shape[0]
    capacity = send_ref.shape[1] - 1
    for p in range(peers):
        send_ref[p, 0:capacity, :] = send[p * capacity:(p + 1) * capacity]
        send_ref[p, capacity:capacity + 1, :] = term_row


def run_block(amps, expo, slot_index, returned, observed, weight, interp, slope_map, tall, main, prev, nxt, peers):
    width, rows = observed.shape
    slots = returned.shape[0]
    comps = tall.shape[0]
    swap = lambda a: jnp.swapaxes(a, -1, -2)
    vm = pl.BlockSpec(memory_space=pltpu.VMEM)
    sm = pl.BlockSpec(memory_space=pltpu.SMEM)
    return pl.pallas_call(
        block_kernel,
        out_shape=jax.ShapeDtypeStruct((peers, slots // peers + 1, rows), jnp.bfloat16),
        in_specs=[sm, sm] + [vm] * 16,
        out_specs=vm,
        scratch_shapes=[pltpu.VMEM((comps, width, rows), jnp.float32)],
    )(amps, expo, slot_index[:, None], slot_index[None, :], returned, observed, weight, interp,
      swap(interp), slope_map, swap(tall), tall, main, prev, nxt, swap(main), swap(prev), swap(nxt))


def body(
    sky_model,
    observed,
    row_weight,
    foot_owner,
    foot_local,
    row_offset,
    exposure_of,
    amplitude,
    subpixel_shift,
    column_profile,
    row_profile,
):
    tile_count = lax.axis_size("tile")
    seg_count = sky_model.shape[1]
    block_rows = sky_model.shape[2]
    block_count = observed.shape[1]
    width = observed.shape[2]
    capacity = 2 * block_count * width // tile_count
    expo_count = amplitude.shape[1]
    comp_count = amplitude.shape[0]
    tile_blocks = width // block_rows
    requests = block_count * width
    pixels = width * block_rows
    highest = lax.Precision.HIGHEST
    bfloat = jnp.bfloat16
    single = jnp.float32
    request_owner = foot_owner.reshape(requests)
    request_local = foot_local.reshape(requests)
    owner_hits = (
        request_owner.reshape(block_count, width)[:, :, None]
        == jnp.arange(tile_count, dtype=jnp.int32)[None, None, :]
    )
    owner_onehot = owner_hits.astype(bfloat)
    within = jnp.einsum(
        "uy,byt->but", strict_lower(width), owner_onehot, preferred_element_type=single
    )
    if block_count > 1:
        block_totals = jnp.sum(owner_onehot.astype(single), axis=1)
        before = jnp.dot(strict_lower(block_count).astype(single), block_totals, precision=highest)
        within = within + before[:, None, :]
    rank_table = jnp.where(owner_hits, within, jnp.zeros((), single))
    owner_rank = jnp.sum(rank_table, axis=2).astype(jnp.int32).reshape(requests)
    slot_index = request_owner * capacity + owner_rank
    slot_iota = jnp.arange(tile_count * capacity, dtype=jnp.int32)
    slot_onehot_t = (slot_iota[:, None] == slot_index[None, :]).astype(bfloat)
    request_code = request_local + 1
    request_parts = jnp.stack([request_code // 32, request_code % 32], axis=1).astype(bfloat)
    request_sums = jnp.dot(slot_onehot_t, request_parts, preferred_element_type=single)
    request_ids = (
        request_sums[:, 0].astype(jnp.int32) * 32 + request_sums[:, 1].astype(jnp.int32)
    ).reshape(tile_count, capacity)
    block_offset = row_offset.reshape(block_count)
    block_exposure = exposure_of.reshape(block_count)
    served_ids = lax.all_to_all(request_ids, "tile", split_axis=0, concat_axis=0, tiled=True)
    served_valid = served_ids > 0
    served_where = jnp.maximum(served_ids - 1, 0)
    local_sky = sky_model[0]
    served_flat = served_ids.reshape(tile_count * capacity) - 1
    seg_iota = jnp.arange(seg_count, dtype=jnp.int32)
    serve_onehot = (served_flat[:, None] == seg_iota[None, :]).astype(bfloat)
    picked_rows = jnp.dot(serve_onehot, local_sky, preferred_element_type=single).astype(bfloat)
    served_rows = picked_rows.reshape(tile_count, capacity, block_rows)
    returned = lax.all_to_all(served_rows, "tile", split_axis=0, concat_axis=0, tiled=True)
    expo_onehot = (
        block_exposure[:, None] == jnp.arange(expo_count, dtype=jnp.int32)[None, :]
    ).astype(single)
    block_amp = jnp.dot(expo_onehot, amplitude.T, precision=highest)
    block_frac = jnp.dot(expo_onehot, subpixel_shift, precision=highest)
    block_wide = jnp.einsum("be,eqt->bqt", expo_onehot, column_profile, precision=highest)
    block_tall = jnp.einsum("be,eqt->bqt", expo_onehot, row_profile, precision=highest)
    j_index = jnp.arange(block_rows, dtype=jnp.int32)[None, :, None]
    v_index = jnp.arange(block_rows, dtype=jnp.int32)[None, None, :]
    offsets = block_offset[:, None, None]
    lower_hit = j_index == v_index + offsets
    upper_hit = j_index == v_index + offsets + 1
    zero_b = jnp.zeros((), bfloat)
    weight_low = (1.0 - block_frac).astype(bfloat)[:, None, None]
    weight_high = block_frac.astype(bfloat)[:, None, None]
    interp = jnp.where(lower_hit, weight_low, zero_b) + jnp.where(upper_hit, weight_high, zero_b)
    slope_map = upper_hit.astype(bfloat) - lower_hit.astype(bfloat)
    tall_kernel = band_lookup(block_tall.astype(bfloat), 0, block_rows)
    wide_profile_b = block_wide.astype(bfloat)
    wide_main = band_lookup(wide_profile_b, 0, block_rows)
    wide_prev = band_lookup(wide_profile_b, -block_rows, block_rows)
    wide_next = band_lookup(wide_profile_b, block_rows, block_rows)
    weight_rows = row_weight.reshape(block_count, block_rows)
    observed_blocks = observed[0]
    returned_rows = returned.reshape(tile_count * capacity, block_rows)
    assert block_count == 1
    term_count = comp_count + 1
    send_all = run_block(
        block_amp[0],
        block_exposure,
        slot_index,
        returned_rows,
        observed_blocks[0],
        weight_rows[0][None, :],
        interp[0],
        slope_map[0],
        tall_kernel[0],
        wide_main[0],
        wide_prev[0],
        wide_next[0],
        tile_count,
    )
    received = lax.all_to_all(send_all, "tile", split_axis=0, concat_axis=0, tiled=True)
    segment_rows = received[:, :capacity]
    peer_rows = received[:, capacity, :].astype(single)
    peer_terms = peer_rows[:, :term_count] + peer_rows[:, LOW_LANE : LOW_LANE + term_count]
    peer_onehot = (
        peer_rows[:, EXPO_LANE][:, None] == jnp.arange(expo_count, dtype=single)[None, :]
    ).astype(single)
    partial_params = jnp.dot(peer_terms.T, peer_onehot, precision=highest)
    flat_rows = segment_rows.reshape(tile_count * capacity, block_rows)
    serve_onehot_t = (seg_iota[:, None] == served_flat[None, :]).astype(bfloat)
    grad_local = jnp.dot(serve_onehot_t, flat_rows, preferred_element_type=single)
    grad_params = lax.psum(partial_params, "band")
    return (grad_local[None], grad_params)


def solution(mesh):
    placed = (
        P("band", "tile", None),
        P("band", "tile", None, None),
        P("band", "tile", None),
        P("band", "tile", None, None),
        P("band", "tile", None),
        P("band", "tile"),
        P("band", "tile"),
        P(),
        P(),
        P(),
        P(),
    )
    return jax.shard_map(
        body, mesh=mesh, in_specs=placed, out_specs=(P("band", "tile", None), P()), check_vma=False
    )
```

```python
import jax
import jax.numpy as jnp
from jax import lax
from jax.sharding import PartitionSpec as P
from jax.experimental import pallas as pl
from jax.experimental.pallas import tpu as pltpu


def band_lookup(profile, lag_shift, size):
    taps = profile.shape[-1]
    out_index = jnp.arange(size, dtype=jnp.int32)[:, None]
    in_index = jnp.arange(size, dtype=jnp.int32)[None, :]
    lag = in_index - out_index + taps // 2 + lag_shift
    tap_mask = (lag[:, :, None] == jnp.arange(taps, dtype=jnp.int32)[None, None, :]).astype(
        jnp.bfloat16
    )
    return jnp.einsum(
        "vwt,bqt->bqvw", tap_mask, profile, preferred_element_type=jnp.float32
    ).astype(jnp.bfloat16)


def from_previous(values):
    blank = jnp.zeros_like(values[:, :, :1])
    return jnp.concatenate([blank, values[:, :, :-1]], axis=2)


def from_next(values):
    blank = jnp.zeros_like(values[:, :, :1])
    return jnp.concatenate([values[:, :, 1:], blank], axis=2)


def strict_lower(size):
    above = jnp.arange(size, dtype=jnp.int32)[:, None]
    below = jnp.arange(size, dtype=jnp.int32)[None, :]
    return (below < above).astype(jnp.bfloat16)


LOW_LANE = 32
EXPO_LANE = 64


def block_kernel(
    amp_ref, expo_ref, slot_col_ref, slot_row_ref, returned_ref, observed_ref, weight_ref, interp_ref,
    interp_t_ref, slope_ref, tall_t_ref, tall_ref, main_ref, prev_ref, next_ref, main_t_ref,
    prev_t_ref, next_t_ref, send_ref, comp_ref,
):
    single = jnp.float32
    bfloat = jnp.bfloat16
    comps = tall_ref.shape[0]
    rows = tall_ref.shape[1]
    width = observed_ref.shape[0]
    slots = returned_ref.shape[0]
    tiles = width // rows
    pick = (
        slot_col_ref[...] == lax.broadcasted_iota(jnp.int32, (width, slots), 1)
    ).astype(bfloat)
    fetched = jnp.dot(pick, returned_ref[...], preferred_element_type=single).astype(bfloat)
    resampled = jnp.dot(fetched, interp_ref[...], preferred_element_type=single).astype(bfloat)
    model = jnp.zeros((width, rows), single)
    for q in range(comps):
        blurred = jnp.dot(resampled, tall_t_ref[q], preferred_element_type=single).astype(bfloat)
        parts = []
        for i in range(tiles):
            acc = jnp.dot(main_ref[q], blurred[i * rows:(i + 1) * rows], preferred_element_type=single)
            if i > 0:
                acc = acc + jnp.dot(prev_ref[q], blurred[(i - 1) * rows:i * rows], preferred_element_type=single)
            if i < tiles - 1:
                acc = acc + jnp.dot(next_ref[q], blurred[(i + 1) * rows:(i + 2) * rows], preferred_element_type=single)
            parts.append(acc)
        component = jnp.concatenate(parts, axis=0)
        comp_ref[q] = component
        model = model + amp_ref[q] * component
    weighted = weight_ref[...] * (model - observed_ref[...].astype(single))
    residual = weighted.astype(bfloat)
    lane = lax.broadcasted_iota(jnp.int32, (1, rows), 1)
    scale = 1.0 / (width * rows)

    def put(terms, total, k):
        total = total * scale
        high = total.astype(bfloat).astype(single)
        low = total - high
        terms = terms + jnp.where(lane == k, high, 0.0)
        return terms + jnp.where(lane == LOW_LANE + k, low, 0.0)

    terms = jnp.zeros((1, rows), single)
    adjoint = jnp.zeros((width, rows), single)
    for q in range(comps):
        amp_sum = jnp.sum(comp_ref[q] * weighted, keepdims=True)
        terms = put(terms, amp_sum, q)
        parts = []
        for i in range(tiles):
            acc = jnp.dot(main_t_ref[q], residual[i * rows:(i + 1) * rows], preferred_element_type=single)
            if i < tiles - 1:
                acc = acc + jnp.dot(prev_t_ref[q], residual[(i + 1) * rows:(i + 2) * rows], preferred_element_type=single)
            if i > 0:
                acc = acc + jnp.dot(next_t_ref[q], residual[(i - 1) * rows:i * rows], preferred_element_type=single)
            parts.append(acc.astype(bfloat))
        back_wide = jnp.concatenate(parts, axis=0)
        adjoint = adjoint + amp_ref[q] * jnp.dot(back_wide, tall_ref[q], preferred_element_type=single)
    slope = jnp.dot(fetched, slope_ref[...], preferred_element_type=single)
    shift_sum = jnp.sum(adjoint * slope, keepdims=True)
    terms = put(terms, shift_sum, comps)
    terms = terms + jnp.where(lane == EXPO_LANE, expo_ref[0].astype(single), 0.0)
    term_row = terms.astype(bfloat)
    grad = jnp.dot(adjoint.astype(bfloat), interp_t_ref[...], preferred_element_type=single).astype(bfloat)
    place = (
        lax.broadcasted_iota(jnp.int32, (slots, width), 0) == slot_row_ref[...]
    ).astype(bfloat)
    send = jnp.dot(place, grad, preferred_element_type=single).astype(bfloat)
    peers = send_ref.shape[0]
    capacity = send_ref.shape[1] - 1
    for p in range(peers):
        send_ref[p, 0:capacity, :] = send[p * capacity:(p + 1) * capacity]
        send_ref[p, capacity:capacity + 1, :] = term_row


def run_block(amps, expo, slot_index, returned, observed, weight, interp, slope_map, tall, main, prev, nxt, peers):
    width, rows = observed.shape
    slots = returned.shape[0]
    comps = tall.shape[0]
    swap = lambda a: jnp.swapaxes(a, -1, -2)
    vm = pl.BlockSpec(memory_space=pltpu.VMEM)
    sm = pl.BlockSpec(memory_space=pltpu.SMEM)
    return pl.pallas_call(
        block_kernel,
        out_shape=jax.ShapeDtypeStruct((peers, slots // peers + 1, rows), jnp.bfloat16),
        in_specs=[sm, sm] + [vm] * 16,
        out_specs=vm,
        scratch_shapes=[pltpu.VMEM((comps, width, rows), jnp.float32)],
    )(amps, expo, slot_index[:, None], slot_index[None, :], returned, observed, weight, interp,
      swap(interp), slope_map, swap(tall), tall, main, prev, nxt, swap(main), swap(prev), swap(nxt))


def body(
    sky_model,
    observed,
    row_weight,
    foot_owner,
    foot_local,
    row_offset,
    exposure_of,
    amplitude,
    subpixel_shift,
    column_profile,
    row_profile,
):
    tile_count = lax.axis_size("tile")
    seg_count = sky_model.shape[1]
    block_rows = sky_model.shape[2]
    block_count = observed.shape[1]
    width = observed.shape[2]
    capacity = 2 * block_count * width // tile_count
    expo_count = amplitude.shape[1]
    comp_count = amplitude.shape[0]
    tile_blocks = width // block_rows
    requests = block_count * width
    pixels = width * block_rows
    highest = lax.Precision.HIGHEST
    bfloat = jnp.bfloat16
    single = jnp.float32
    request_owner = foot_owner.reshape(requests)
    request_local = foot_local.reshape(requests)
    owner_hits = (
        request_owner.reshape(block_count, width)[:, :, None]
        == jnp.arange(tile_count, dtype=jnp.int32)[None, None, :]
    )
    owner_onehot = owner_hits.astype(bfloat)
    within = jnp.einsum(
        "uy,byt->but", strict_lower(width), owner_onehot, preferred_element_type=single
    )
    if block_count > 1:
        block_totals = jnp.sum(owner_onehot.astype(single), axis=1)
        before = jnp.dot(strict_lower(block_count).astype(single), block_totals, precision=highest)
        within = within + before[:, None, :]
    rank_table = jnp.where(owner_hits, within, jnp.zeros((), single))
    owner_rank = jnp.sum(rank_table, axis=2).astype(jnp.int32).reshape(requests)
    slot_index = request_owner * capacity + owner_rank
    slot_iota = jnp.arange(tile_count * capacity, dtype=jnp.int32)
    slot_onehot = (slot_index[:, None] == slot_iota[None, :]).astype(bfloat)
    request_code = request_local + 1
    request_parts = jnp.stack([request_code // 32, request_code % 32]).astype(bfloat)
    request_sums = jnp.dot(request_parts, slot_onehot, preferred_element_type=single)
    request_ids = (
        request_sums[0].astype(jnp.int32) * 32 + request_sums[1].astype(jnp.int32)
    ).reshape(tile_count, capacity)
    block_offset = row_offset.reshape(block_count)
    block_exposure = exposure_of.reshape(block_count)
    served_ids = lax.all_to_all(request_ids, "tile", split_axis=0, concat_axis=0, tiled=True)
    served_valid = served_ids > 0
    served_where = jnp.maximum(served_ids - 1, 0)
    local_sky = sky_model[0]
    served_flat = served_ids.reshape(tile_count * capacity) - 1
    seg_iota = jnp.arange(seg_count, dtype=jnp.int32)
    serve_onehot = (served_flat[:, None] == seg_iota[None, :]).astype(bfloat)
    picked_rows = jnp.dot(serve_onehot, local_sky, preferred_element_type=single).astype(bfloat)
    served_rows = picked_rows.reshape(tile_count, capacity, block_rows)
    returned = lax.all_to_all(served_rows, "tile", split_axis=0, concat_axis=0, tiled=True)
    expo_onehot = (
        block_exposure[:, None] == jnp.arange(expo_count, dtype=jnp.int32)[None, :]
    ).astype(single)
    block_amp = jnp.dot(expo_onehot, amplitude.T, precision=highest)
    block_frac = jnp.dot(expo_onehot, subpixel_shift, precision=highest)
    block_wide = jnp.einsum("be,eqt->bqt", expo_onehot, column_profile, precision=highest)
    block_tall = jnp.einsum("be,eqt->bqt", expo_onehot, row_profile, precision=highest)
    j_index = jnp.arange(block_rows, dtype=jnp.int32)[None, :, None]
    v_index = jnp.arange(block_rows, dtype=jnp.int32)[None, None, :]
    offsets = block_offset[:, None, None]
    lower_hit = j_index == v_index + offsets
    upper_hit = j_index == v_index + offsets + 1
    zero_b = jnp.zeros((), bfloat)
    weight_low = (1.0 - block_frac).astype(bfloat)[:, None, None]
    weight_high = block_frac.astype(bfloat)[:, None, None]
    interp = jnp.where(lower_hit, weight_low, zero_b) + jnp.where(upper_hit, weight_high, zero_b)
    slope_map = upper_hit.astype(bfloat) - lower_hit.astype(bfloat)
    tall_kernel = band_lookup(block_tall.astype(bfloat), 0, block_rows)
    wide_profile_b = block_wide.astype(bfloat)
    wide_main = band_lookup(wide_profile_b, 0, block_rows)
    wide_prev = band_lookup(wide_profile_b, -block_rows, block_rows)
    wide_next = band_lookup(wide_profile_b, block_rows, block_rows)
    weight_rows = row_weight.reshape(block_count, block_rows)
    observed_blocks = observed[0]
    returned_rows = returned.reshape(tile_count * capacity, block_rows)
    assert block_count == 1
    term_count = comp_count + 1
    send_all = run_block(
        block_amp[0],
        block_exposure,
        slot_index,
        returned_rows,
        observed_blocks[0],
        weight_rows[0][None, :],
        interp[0],
        slope_map[0],
        tall_kernel[0],
        wide_main[0],
        wide_prev[0],
        wide_next[0],
        tile_count,
    )
    received = lax.all_to_all(send_all, "tile", split_axis=0, concat_axis=0, tiled=True)
    segment_rows = received[:, :capacity]
    peer_rows = received[:, capacity, :].astype(single)
    peer_terms = peer_rows[:, :term_count] + peer_rows[:, LOW_LANE : LOW_LANE + term_count]
    peer_onehot = (
        peer_rows[:, EXPO_LANE][:, None] == jnp.arange(expo_count, dtype=single)[None, :]
    ).astype(single)
    partial_params = jnp.dot(peer_terms.T, peer_onehot, precision=highest)
    flat_rows = segment_rows.reshape(tile_count * capacity, block_rows)
    serve_onehot_t = (seg_iota[:, None] == served_flat[None, :]).astype(bfloat)
    grad_local = jnp.dot(serve_onehot_t, flat_rows, preferred_element_type=single)
    grad_params = lax.psum(partial_params, "band")
    return (grad_local[None], grad_params)


def solution(mesh):
    placed = (
        P("band", "tile", None),
        P("band", "tile", None, None),
        P("band", "tile", None),
        P("band", "tile", None, None),
        P("band", "tile", None),
        P("band", "tile"),
        P("band", "tile"),
        P(),
        P(),
        P(),
        P(),
    )
    return jax.shard_map(
        body, mesh=mesh, in_specs=placed, out_specs=(P("band", "tile", None), P()), check_vma=False
    )
```

```python
import jax
import jax.numpy as jnp
from jax import lax
from jax.sharding import PartitionSpec as P
from jax.experimental import pallas as pl
from jax.experimental.pallas import tpu as pltpu


def band_lookup(profile, lag_shift, size):
    taps = profile.shape[-1]
    out_index = jnp.arange(size, dtype=jnp.int32)[:, None]
    in_index = jnp.arange(size, dtype=jnp.int32)[None, :]
    lag = in_index - out_index + taps // 2 + lag_shift
    tap_mask = (lag[:, :, None] == jnp.arange(taps, dtype=jnp.int32)[None, None, :]).astype(
        jnp.bfloat16
    )
    return jnp.einsum(
        "vwt,bqt->bqvw", tap_mask, profile, preferred_element_type=jnp.float32
    ).astype(jnp.bfloat16)


def from_previous(values):
    blank = jnp.zeros_like(values[:, :, :1])
    return jnp.concatenate([blank, values[:, :, :-1]], axis=2)


def from_next(values):
    blank = jnp.zeros_like(values[:, :, :1])
    return jnp.concatenate([values[:, :, 1:], blank], axis=2)


def strict_lower(size):
    above = jnp.arange(size, dtype=jnp.int32)[:, None]
    below = jnp.arange(size, dtype=jnp.int32)[None, :]
    return (below < above).astype(jnp.bfloat16)


LOW_LANE = 32
EXPO_LANE = 64


def block_kernel(
    amp_ref, expo_ref, slot_col_ref, slot_row_ref, returned_ref, observed_ref, weight_ref, interp_ref,
    interp_t_ref, slope_ref, tall_t_ref, tall_ref, main_ref, prev_ref, next_ref, main_t_ref,
    prev_t_ref, next_t_ref, send_ref, comp_ref, returned_vmem, observed_vmem, copy_sems,
):
    single = jnp.float32
    bfloat = jnp.bfloat16
    comps = tall_ref.shape[0]
    rows = tall_ref.shape[1]
    width = observed_ref.shape[0]
    slots = returned_ref.shape[0]
    tiles = width // rows
    pick = (
        slot_col_ref[...] == lax.broadcasted_iota(jnp.int32, (width, slots), 1)
    ).astype(bfloat)
    returned_copy = pltpu.make_async_copy(returned_ref, returned_vmem, copy_sems.at[0])
    observed_copy = pltpu.make_async_copy(observed_ref, observed_vmem, copy_sems.at[1])
    returned_copy.start()
    observed_copy.start()
    returned_copy.wait()
    fetched = jnp.dot(pick, returned_vmem[...], preferred_element_type=single).astype(bfloat)
    resampled = jnp.dot(fetched, interp_ref[...], preferred_element_type=single).astype(bfloat)
    model = jnp.zeros((width, rows), single)
    for q in range(comps):
        blurred = jnp.dot(resampled, tall_t_ref[q], preferred_element_type=single).astype(bfloat)
        parts = []
        for i in range(tiles):
            acc = jnp.dot(main_ref[q], blurred[i * rows:(i + 1) * rows], preferred_element_type=single)
            if i > 0:
                acc = acc + jnp.dot(prev_ref[q], blurred[(i - 1) * rows:i * rows], preferred_element_type=single)
            if i < tiles - 1:
                acc = acc + jnp.dot(next_ref[q], blurred[(i + 1) * rows:(i + 2) * rows], preferred_element_type=single)
            parts.append(acc)
        component = jnp.concatenate(parts, axis=0)
        comp_ref[q] = component
        model = model + amp_ref[q] * component
    observed_copy.wait()
    weighted = weight_ref[...] * (model - observed_vmem[...].astype(single))
    residual = weighted.astype(bfloat)
    lane = lax.broadcasted_iota(jnp.int32, (1, rows), 1)
    scale = 1.0 / (width * rows)

    def put(terms, total, k):
        total = total * scale
        high = total.astype(bfloat).astype(single)
        low = total - high
        terms = terms + jnp.where(lane == k, high, 0.0)
        return terms + jnp.where(lane == LOW_LANE + k, low, 0.0)

    terms = jnp.zeros((1, rows), single)
    adjoint = jnp.zeros((width, rows), single)
    for q in range(comps):
        amp_sum = jnp.sum(comp_ref[q] * weighted, keepdims=True)
        terms = put(terms, amp_sum, q)
        parts = []
        for i in range(tiles):
            acc = jnp.dot(main_t_ref[q], residual[i * rows:(i + 1) * rows], preferred_element_type=single)
            if i < tiles - 1:
                acc = acc + jnp.dot(prev_t_ref[q], residual[(i + 1) * rows:(i + 2) * rows], preferred_element_type=single)
            if i > 0:
                acc = acc + jnp.dot(next_t_ref[q], residual[(i - 1) * rows:i * rows], preferred_element_type=single)
            parts.append(acc.astype(bfloat))
        back_wide = jnp.concatenate(parts, axis=0)
        adjoint = adjoint + amp_ref[q] * jnp.dot(back_wide, tall_ref[q], preferred_element_type=single)
    slope = jnp.dot(fetched, slope_ref[...], preferred_element_type=single)
    shift_sum = jnp.sum(adjoint * slope, keepdims=True)
    terms = put(terms, shift_sum, comps)
    terms = terms + jnp.where(lane == EXPO_LANE, expo_ref[0].astype(single), 0.0)
    term_row = terms.astype(bfloat)
    grad = jnp.dot(adjoint.astype(bfloat), interp_t_ref[...], preferred_element_type=single).astype(bfloat)
    place = (
        lax.broadcasted_iota(jnp.int32, (slots, width), 0) == slot_row_ref[...]
    ).astype(bfloat)
    send = jnp.dot(place, grad, preferred_element_type=single).astype(bfloat)
    peers = send_ref.shape[0]
    capacity = send_ref.shape[1] - 1
    for p in range(peers):
        send_ref[p, 0:capacity, :] = send[p * capacity:(p + 1) * capacity]
        send_ref[p, capacity:capacity + 1, :] = term_row


def run_block(amps, expo, slot_index, returned, observed, weight, interp, slope_map, tall, main, prev, nxt, peers):
    width, rows = observed.shape
    slots = returned.shape[0]
    comps = tall.shape[0]
    swap = lambda a: jnp.swapaxes(a, -1, -2)
    vm = pl.BlockSpec(memory_space=pltpu.VMEM)
    sm = pl.BlockSpec(memory_space=pltpu.SMEM)
    anywhere = pl.BlockSpec(memory_space=pl.ANY)
    return pl.pallas_call(
        block_kernel,
        out_shape=jax.ShapeDtypeStruct((peers, slots // peers + 1, rows), jnp.bfloat16),
        in_specs=[sm, sm, vm, vm, anywhere, anywhere] + [vm] * 12,
        out_specs=vm,
        scratch_shapes=[
            pltpu.VMEM((comps, width, rows), jnp.float32),
            pltpu.VMEM((slots, rows), jnp.bfloat16),
            pltpu.VMEM((width, rows), jnp.bfloat16),
            pltpu.SemaphoreType.DMA((2,)),
        ],
    )(amps, expo, slot_index[:, None], slot_index[None, :], returned, observed, weight, interp,
      swap(interp), slope_map, swap(tall), tall, main, prev, nxt, swap(main), swap(prev), swap(nxt))


def body(
    sky_model,
    observed,
    row_weight,
    foot_owner,
    foot_local,
    row_offset,
    exposure_of,
    amplitude,
    subpixel_shift,
    column_profile,
    row_profile,
):
    tile_count = lax.axis_size("tile")
    seg_count = sky_model.shape[1]
    block_rows = sky_model.shape[2]
    block_count = observed.shape[1]
    width = observed.shape[2]
    capacity = 2 * block_count * width // tile_count
    expo_count = amplitude.shape[1]
    comp_count = amplitude.shape[0]
    tile_blocks = width // block_rows
    requests = block_count * width
    pixels = width * block_rows
    highest = lax.Precision.HIGHEST
    bfloat = jnp.bfloat16
    single = jnp.float32
    request_owner = foot_owner.reshape(requests)
    request_local = foot_local.reshape(requests)
    owner_hits = (
        request_owner.reshape(block_count, width)[:, :, None]
        == jnp.arange(tile_count, dtype=jnp.int32)[None, None, :]
    )
    owner_onehot = owner_hits.astype(bfloat)
    within = jnp.einsum(
        "uy,byt->but", strict_lower(width), owner_onehot, preferred_element_type=single
    )
    if block_count > 1:
        block_totals = jnp.sum(owner_onehot.astype(single), axis=1)
        before = jnp.dot(strict_lower(block_count).astype(single), block_totals, precision=highest)
        within = within + before[:, None, :]
    rank_table = jnp.where(owner_hits, within, jnp.zeros((), single))
    owner_rank = jnp.sum(rank_table, axis=2).astype(jnp.int32).reshape(requests)
    slot_index = request_owner * capacity + owner_rank
    slot_iota = jnp.arange(tile_count * capacity, dtype=jnp.int32)
    slot_onehot_t = (slot_iota[:, None] == slot_index[None, :]).astype(bfloat)
    request_code = request_local + 1
    request_parts = jnp.stack([request_code // 32, request_code % 32], axis=1).astype(bfloat)
    request_sums = jnp.dot(slot_onehot_t, request_parts, preferred_element_type=single)
    request_ids = (
        request_sums[:, 0].astype(jnp.int32) * 32 + request_sums[:, 1].astype(jnp.int32)
    ).reshape(tile_count, capacity)
    block_offset = row_offset.reshape(block_count)
    block_exposure = exposure_of.reshape(block_count)
    served_ids = lax.all_to_all(request_ids, "tile", split_axis=0, concat_axis=0, tiled=True)
    served_valid = served_ids > 0
    served_where = jnp.maximum(served_ids - 1, 0)
    local_sky = sky_model[0]
    served_flat = served_ids.reshape(tile_count * capacity) - 1
    seg_iota = jnp.arange(seg_count, dtype=jnp.int32)
    serve_onehot = (served_flat[:, None] == seg_iota[None, :]).astype(bfloat)
    picked_rows = jnp.dot(serve_onehot, local_sky, preferred_element_type=single).astype(bfloat)
    served_rows = picked_rows.reshape(tile_count, capacity, block_rows)
    returned = lax.all_to_all(served_rows, "tile", split_axis=0, concat_axis=0, tiled=True)
    expo_onehot = (
        block_exposure[:, None] == jnp.arange(expo_count, dtype=jnp.int32)[None, :]
    ).astype(single)
    block_amp = jnp.dot(expo_onehot, amplitude.T, precision=highest)
    block_frac = jnp.dot(expo_onehot, subpixel_shift, precision=highest)
    block_wide = jnp.einsum("be,eqt->bqt", expo_onehot, column_profile, precision=highest)
    block_tall = jnp.einsum("be,eqt->bqt", expo_onehot, row_profile, precision=highest)
    j_index = jnp.arange(block_rows, dtype=jnp.int32)[None, :, None]
    v_index = jnp.arange(block_rows, dtype=jnp.int32)[None, None, :]
    offsets = block_offset[:, None, None]
    lower_hit = j_index == v_index + offsets
    upper_hit = j_index == v_index + offsets + 1
    zero_b = jnp.zeros((), bfloat)
    weight_low = (1.0 - block_frac).astype(bfloat)[:, None, None]
    weight_high = block_frac.astype(bfloat)[:, None, None]
    interp = jnp.where(lower_hit, weight_low, zero_b) + jnp.where(upper_hit, weight_high, zero_b)
    slope_map = upper_hit.astype(bfloat) - lower_hit.astype(bfloat)
    tall_kernel = band_lookup(block_tall.astype(bfloat), 0, block_rows)
    wide_profile_b = block_wide.astype(bfloat)
    wide_main = band_lookup(wide_profile_b, 0, block_rows)
    wide_prev = band_lookup(wide_profile_b, -block_rows, block_rows)
    wide_next = band_lookup(wide_profile_b, block_rows, block_rows)
    weight_rows = row_weight.reshape(block_count, block_rows)
    observed_blocks = observed[0]
    returned_rows = returned.reshape(tile_count * capacity, block_rows)
    assert block_count == 1
    term_count = comp_count + 1
    send_all = run_block(
        block_amp[0],
        block_exposure,
        slot_index,
        returned_rows,
        observed_blocks[0],
        weight_rows[0][None, :],
        interp[0],
        slope_map[0],
        tall_kernel[0],
        wide_main[0],
        wide_prev[0],
        wide_next[0],
        tile_count,
    )
    received = lax.all_to_all(send_all, "tile", split_axis=0, concat_axis=0, tiled=True)
    segment_rows = received[:, :capacity]
    peer_rows = received[:, capacity, :].astype(single)
    peer_terms = peer_rows[:, :term_count] + peer_rows[:, LOW_LANE : LOW_LANE + term_count]
    peer_onehot = (
        peer_rows[:, EXPO_LANE][:, None] == jnp.arange(expo_count, dtype=single)[None, :]
    ).astype(single)
    partial_params = jnp.dot(peer_terms.T, peer_onehot, precision=highest)
    flat_rows = segment_rows.reshape(tile_count * capacity, block_rows)
    serve_onehot_t = (seg_iota[:, None] == served_flat[None, :]).astype(bfloat)
    grad_local = jnp.dot(serve_onehot_t, flat_rows, preferred_element_type=single)
    grad_params = lax.psum(partial_params, "band")
    return (grad_local[None], grad_params)


def solution(mesh):
    placed = (
        P("band", "tile", None),
        P("band", "tile", None, None),
        P("band", "tile", None),
        P("band", "tile", None, None),
        P("band", "tile", None),
        P("band", "tile"),
        P("band", "tile"),
        P(),
        P(),
        P(),
        P(),
    )
    return jax.shard_map(
        body, mesh=mesh, in_specs=placed, out_specs=(P("band", "tile", None), P()), check_vma=False
    )
```

```python
import jax
import jax.numpy as jnp
from jax import lax
from jax.sharding import PartitionSpec as P
from jax.experimental import pallas as pl
from jax.experimental.pallas import tpu as pltpu


def band_lookup(profile, lag_shift, size):
    taps = profile.shape[-1]
    out_index = jnp.arange(size, dtype=jnp.int32)[:, None]
    in_index = jnp.arange(size, dtype=jnp.int32)[None, :]
    lag = in_index - out_index + taps // 2 + lag_shift
    tap_mask = (lag[:, :, None] == jnp.arange(taps, dtype=jnp.int32)[None, None, :]).astype(
        jnp.bfloat16
    )
    return jnp.einsum(
        "vwt,bqt->bqvw", tap_mask, profile, preferred_element_type=jnp.float32
    ).astype(jnp.bfloat16)


def from_previous(values):
    blank = jnp.zeros_like(values[:, :, :1])
    return jnp.concatenate([blank, values[:, :, :-1]], axis=2)


def from_next(values):
    blank = jnp.zeros_like(values[:, :, :1])
    return jnp.concatenate([values[:, :, 1:], blank], axis=2)


def strict_lower(size):
    above = jnp.arange(size, dtype=jnp.int32)[:, None]
    below = jnp.arange(size, dtype=jnp.int32)[None, :]
    return (below < above).astype(jnp.bfloat16)


LOW_LANE = 32
EXPO_LANE = 64


def block_kernel(
    amp_ref, expo_ref, pick_ref, place_ref, returned_ref, observed_ref, weight_ref, interp_ref,
    interp_t_ref, slope_ref, tall_t_ref, tall_ref, main_ref, prev_ref, next_ref, main_t_ref,
    prev_t_ref, next_t_ref, send_ref, comp_ref, pick_vmem, place_vmem, copy_sems,
):
    single = jnp.float32
    bfloat = jnp.bfloat16
    comps = tall_ref.shape[0]
    rows = tall_ref.shape[1]
    width = observed_ref.shape[0]
    slots = returned_ref.shape[0]
    tiles = width // rows
    pick_copy = pltpu.make_async_copy(pick_ref, pick_vmem, copy_sems.at[0])
    place_copy = pltpu.make_async_copy(place_ref, place_vmem, copy_sems.at[1])
    pick_copy.start()
    place_copy.start()
    pick_copy.wait()
    fetched = jnp.dot(pick_vmem[...], returned_ref[...], preferred_element_type=single).astype(bfloat)
    resampled = jnp.dot(fetched, interp_ref[...], preferred_element_type=single).astype(bfloat)
    model = jnp.zeros((width, rows), single)
    for q in range(comps):
        blurred = jnp.dot(resampled, tall_t_ref[q], preferred_element_type=single).astype(bfloat)
        parts = []
        for i in range(tiles):
            acc = jnp.dot(main_ref[q], blurred[i * rows:(i + 1) * rows], preferred_element_type=single)
            if i > 0:
                acc = acc + jnp.dot(prev_ref[q], blurred[(i - 1) * rows:i * rows], preferred_element_type=single)
            if i < tiles - 1:
                acc = acc + jnp.dot(next_ref[q], blurred[(i + 1) * rows:(i + 2) * rows], preferred_element_type=single)
            parts.append(acc)
        component = jnp.concatenate(parts, axis=0)
        comp_ref[q] = component
        model = model + amp_ref[q] * component
    weighted = weight_ref[...] * (model - observed_ref[...].astype(single))
    residual = weighted.astype(bfloat)
    lane = lax.broadcasted_iota(jnp.int32, (1, rows), 1)
    scale = 1.0 / (width * rows)

    def put(terms, total, k):
        total = total * scale
        high = total.astype(bfloat).astype(single)
        low = total - high
        terms = terms + jnp.where(lane == k, high, 0.0)
        return terms + jnp.where(lane == LOW_LANE + k, low, 0.0)

    terms = jnp.zeros((1, rows), single)
    adjoint = jnp.zeros((width, rows), single)
    for q in range(comps):
        amp_sum = jnp.sum(comp_ref[q] * weighted, keepdims=True)
        terms = put(terms, amp_sum, q)
        parts = []
        for i in range(tiles):
            acc = jnp.dot(main_t_ref[q], residual[i * rows:(i + 1) * rows], preferred_element_type=single)
            if i < tiles - 1:
                acc = acc + jnp.dot(prev_t_ref[q], residual[(i + 1) * rows:(i + 2) * rows], preferred_element_type=single)
            if i > 0:
                acc = acc + jnp.dot(next_t_ref[q], residual[(i - 1) * rows:i * rows], preferred_element_type=single)
            parts.append(acc.astype(bfloat))
        back_wide = jnp.concatenate(parts, axis=0)
        adjoint = adjoint + amp_ref[q] * jnp.dot(back_wide, tall_ref[q], preferred_element_type=single)
    slope = jnp.dot(fetched, slope_ref[...], preferred_element_type=single)
    shift_sum = jnp.sum(adjoint * slope, keepdims=True)
    terms = put(terms, shift_sum, comps)
    terms = terms + jnp.where(lane == EXPO_LANE, expo_ref[0].astype(single), 0.0)
    term_row = terms.astype(bfloat)
    grad = jnp.dot(adjoint.astype(bfloat), interp_t_ref[...], preferred_element_type=single).astype(bfloat)
    place_copy.wait()
    send = jnp.dot(place_vmem[...], grad, preferred_element_type=single).astype(bfloat)
    peers = send_ref.shape[0]
    capacity = send_ref.shape[1] - 1
    for p in range(peers):
        send_ref[p, 0:capacity, :] = send[p * capacity:(p + 1) * capacity]
        send_ref[p, capacity:capacity + 1, :] = term_row


def run_block(amps, expo, slot_index, returned, observed, weight, interp, slope_map, tall, main, prev, nxt, peers):
    width, rows = observed.shape
    slots = returned.shape[0]
    comps = tall.shape[0]
    swap = lambda a: jnp.swapaxes(a, -1, -2)
    vm = pl.BlockSpec(memory_space=pltpu.VMEM)
    sm = pl.BlockSpec(memory_space=pltpu.SMEM)
    anywhere = pl.BlockSpec(memory_space=pl.ANY)
    pick = (
        slot_index[:, None] == jnp.arange(slots, dtype=jnp.int32)[None, :]
    ).astype(jnp.bfloat16)
    return pl.pallas_call(
        block_kernel,
        out_shape=jax.ShapeDtypeStruct((peers, slots // peers + 1, rows), jnp.bfloat16),
        in_specs=[sm, sm, anywhere, anywhere] + [vm] * 14,
        out_specs=vm,
        scratch_shapes=[
            pltpu.VMEM((comps, width, rows), jnp.float32),
            pltpu.VMEM((width, slots), jnp.bfloat16),
            pltpu.VMEM((slots, width), jnp.bfloat16),
            pltpu.SemaphoreType.DMA((2,)),
        ],
    )(amps, expo, pick, pick.T, returned, observed, weight, interp,
      swap(interp), slope_map, swap(tall), tall, main, prev, nxt, swap(main), swap(prev), swap(nxt))


def body(
    sky_model,
    observed,
    row_weight,
    foot_owner,
    foot_local,
    row_offset,
    exposure_of,
    amplitude,
    subpixel_shift,
    column_profile,
    row_profile,
):
    tile_count = lax.axis_size("tile")
    seg_count = sky_model.shape[1]
    block_rows = sky_model.shape[2]
    block_count = observed.shape[1]
    width = observed.shape[2]
    capacity = 2 * block_count * width // tile_count
    expo_count = amplitude.shape[1]
    comp_count = amplitude.shape[0]
    tile_blocks = width // block_rows
    requests = block_count * width
    pixels = width * block_rows
    highest = lax.Precision.HIGHEST
    bfloat = jnp.bfloat16
    single = jnp.float32
    request_owner = foot_owner.reshape(requests)
    request_local = foot_local.reshape(requests)
    owner_hits = (
        request_owner.reshape(block_count, width)[:, :, None]
        == jnp.arange(tile_count, dtype=jnp.int32)[None, None, :]
    )
    owner_onehot = owner_hits.astype(bfloat)
    within = jnp.einsum(
        "uy,byt->but", strict_lower(width), owner_onehot, preferred_element_type=single
    )
    if block_count > 1:
        block_totals = jnp.sum(owner_onehot.astype(single), axis=1)
        before = jnp.dot(strict_lower(block_count).astype(single), block_totals, precision=highest)
        within = within + before[:, None, :]
    rank_table = jnp.where(owner_hits, within, jnp.zeros((), single))
    owner_rank = jnp.sum(rank_table, axis=2).astype(jnp.int32).reshape(requests)
    slot_index = request_owner * capacity + owner_rank
    slot_iota = jnp.arange(tile_count * capacity, dtype=jnp.int32)
    slot_onehot_t = (slot_iota[:, None] == slot_index[None, :]).astype(bfloat)
    request_code = request_local + 1
    request_parts = jnp.stack([request_code // 32, request_code % 32], axis=1).astype(bfloat)
    request_sums = jnp.dot(slot_onehot_t, request_parts, preferred_element_type=single)
    request_ids = (
        request_sums[:, 0].astype(jnp.int32) * 32 + request_sums[:, 1].astype(jnp.int32)
    ).reshape(tile_count, capacity)
    block_offset = row_offset.reshape(block_count)
    block_exposure = exposure_of.reshape(block_count)
    served_ids = lax.all_to_all(request_ids, "tile", split_axis=0, concat_axis=0, tiled=True)
    served_valid = served_ids > 0
    served_where = jnp.maximum(served_ids - 1, 0)
    local_sky = sky_model[0]
    served_flat = served_ids.reshape(tile_count * capacity) - 1
    seg_iota = jnp.arange(seg_count, dtype=jnp.int32)
    serve_onehot = (served_flat[:, None] == seg_iota[None, :]).astype(bfloat)
    picked_rows = jnp.dot(serve_onehot, local_sky, preferred_element_type=single).astype(bfloat)
    served_rows = picked_rows.reshape(tile_count, capacity, block_rows)
    returned = lax.all_to_all(served_rows, "tile", split_axis=0, concat_axis=0, tiled=True)
    expo_onehot = (
        block_exposure[:, None] == jnp.arange(expo_count, dtype=jnp.int32)[None, :]
    ).astype(single)
    block_amp = jnp.dot(expo_onehot, amplitude.T, precision=highest)
    block_frac = jnp.dot(expo_onehot, subpixel_shift, precision=highest)
    block_wide = jnp.einsum("be,eqt->bqt", expo_onehot, column_profile, precision=highest)
    block_tall = jnp.einsum("be,eqt->bqt", expo_onehot, row_profile, precision=highest)
    j_index = jnp.arange(block_rows, dtype=jnp.int32)[None, :, None]
    v_index = jnp.arange(block_rows, dtype=jnp.int32)[None, None, :]
    offsets = block_offset[:, None, None]
    lower_hit = j_index == v_index + offsets
    upper_hit = j_index == v_index + offsets + 1
    zero_b = jnp.zeros((), bfloat)
    weight_low = (1.0 - block_frac).astype(bfloat)[:, None, None]
    weight_high = block_frac.astype(bfloat)[:, None, None]
    interp = jnp.where(lower_hit, weight_low, zero_b) + jnp.where(upper_hit, weight_high, zero_b)
    slope_map = upper_hit.astype(bfloat) - lower_hit.astype(bfloat)
    tall_kernel = band_lookup(block_tall.astype(bfloat), 0, block_rows)
    wide_profile_b = block_wide.astype(bfloat)
    wide_main = band_lookup(wide_profile_b, 0, block_rows)
    wide_prev = band_lookup(wide_profile_b, -block_rows, block_rows)
    wide_next = band_lookup(wide_profile_b, block_rows, block_rows)
    weight_rows = row_weight.reshape(block_count, block_rows)
    observed_blocks = observed[0]
    returned_rows = returned.reshape(tile_count * capacity, block_rows)
    assert block_count == 1
    term_count = comp_count + 1
    send_all = run_block(
        block_amp[0],
        block_exposure,
        slot_index,
        returned_rows,
        observed_blocks[0],
        weight_rows[0][None, :],
        interp[0],
        slope_map[0],
        tall_kernel[0],
        wide_main[0],
        wide_prev[0],
        wide_next[0],
        tile_count,
    )
    received = lax.all_to_all(send_all, "tile", split_axis=0, concat_axis=0, tiled=True)
    segment_rows = received[:, :capacity]
    peer_rows = received[:, capacity, :].astype(single)
    peer_terms = peer_rows[:, :term_count] + peer_rows[:, LOW_LANE : LOW_LANE + term_count]
    peer_onehot = (
        peer_rows[:, EXPO_LANE][:, None] == jnp.arange(expo_count, dtype=single)[None, :]
    ).astype(single)
    partial_params = jnp.dot(peer_terms.T, peer_onehot, precision=highest)
    flat_rows = segment_rows.reshape(tile_count * capacity, block_rows)
    serve_onehot_t = (seg_iota[:, None] == served_flat[None, :]).astype(bfloat)
    grad_local = jnp.dot(serve_onehot_t, flat_rows, preferred_element_type=single)
    grad_params = lax.psum(partial_params, "band")
    return (grad_local[None], grad_params)


def solution(mesh):
    placed = (
        P("band", "tile", None),
        P("band", "tile", None, None),
        P("band", "tile", None),
        P("band", "tile", None, None),
        P("band", "tile", None),
        P("band", "tile"),
        P("band", "tile"),
        P(),
        P(),
        P(),
        P(),
    )
    return jax.shard_map(
        body, mesh=mesh, in_specs=placed, out_specs=(P("band", "tile", None), P()), check_vma=False
    )
```

```python
import jax
import jax.numpy as jnp
from jax import lax
from jax.sharding import PartitionSpec as P
from jax.experimental import pallas as pl
from jax.experimental.pallas import tpu as pltpu


def band_lookup(profile, lag_shift, size):
    taps = profile.shape[-1]
    out_index = jnp.arange(size, dtype=jnp.int32)[:, None]
    in_index = jnp.arange(size, dtype=jnp.int32)[None, :]
    lag = in_index - out_index + taps // 2 + lag_shift
    tap_mask = (lag[:, :, None] == jnp.arange(taps, dtype=jnp.int32)[None, None, :]).astype(
        jnp.bfloat16
    )
    return jnp.einsum(
        "vwt,bqt->bqvw", tap_mask, profile, preferred_element_type=jnp.float32
    ).astype(jnp.bfloat16)


def from_previous(values):
    blank = jnp.zeros_like(values[:, :, :1])
    return jnp.concatenate([blank, values[:, :, :-1]], axis=2)


def from_next(values):
    blank = jnp.zeros_like(values[:, :, :1])
    return jnp.concatenate([values[:, :, 1:], blank], axis=2)


def strict_lower(size):
    above = jnp.arange(size, dtype=jnp.int32)[:, None]
    below = jnp.arange(size, dtype=jnp.int32)[None, :]
    return (below < above).astype(jnp.bfloat16)


LOW_LANE = 32
EXPO_LANE = 64


def block_kernel(
    amp_ref, expo_ref, slot_col_ref, slot_row_ref, returned_ref, observed_ref, weight_ref, interp_ref,
    interp_t_ref, slope_ref, tall_t_ref, tall_ref, main_ref, prev_ref, next_ref, main_t_ref,
    prev_t_ref, next_t_ref, send_ref, comp_ref,
):
    single = jnp.float32
    bfloat = jnp.bfloat16
    comps = tall_ref.shape[0]
    rows = tall_ref.shape[1]
    width = observed_ref.shape[0]
    slots = returned_ref.shape[0]
    tiles = width // rows
    pick = (
        slot_col_ref[...] == lax.broadcasted_iota(jnp.int32, (width, slots), 1)
    ).astype(bfloat)
    fetched = jnp.dot(pick, returned_ref[...], preferred_element_type=single).astype(bfloat)
    resampled = jnp.dot(fetched, interp_ref[...], preferred_element_type=single).astype(bfloat)
    model = jnp.zeros((width, rows), single)
    for q in range(comps):
        blurred = jnp.dot(resampled, tall_t_ref[q], preferred_element_type=single).astype(bfloat)
        parts = []
        for i in range(tiles):
            acc = jnp.dot(main_ref[q], blurred[i * rows:(i + 1) * rows], preferred_element_type=single)
            if i > 0:
                acc = acc + jnp.dot(prev_ref[q], blurred[(i - 1) * rows:i * rows], preferred_element_type=single)
            if i < tiles - 1:
                acc = acc + jnp.dot(next_ref[q], blurred[(i + 1) * rows:(i + 2) * rows], preferred_element_type=single)
            parts.append(acc)
        component = jnp.concatenate(parts, axis=0)
        comp_ref[q] = component
        model = model + amp_ref[q] * component
    weighted = weight_ref[...] * (model - observed_ref[...].astype(single))
    residual = weighted.astype(bfloat)
    lane = lax.broadcasted_iota(jnp.int32, (1, rows), 1)
    scale = 1.0 / (width * rows)

    def put(terms, total, k):
        total = total * scale
        high = total.astype(bfloat).astype(single)
        low = total - high
        terms = terms + jnp.where(lane == k, high, 0.0)
        return terms + jnp.where(lane == LOW_LANE + k, low, 0.0)

    terms = jnp.zeros((1, rows), single)
    adjoint = jnp.zeros((width, rows), single)
    for q in range(comps):
        amp_sum = jnp.sum(comp_ref[q] * weighted, keepdims=True)
        terms = put(terms, amp_sum, q)
        parts = []
        for i in range(tiles):
            acc = jnp.dot(main_t_ref[q], residual[i * rows:(i + 1) * rows], preferred_element_type=single)
            if i < tiles - 1:
                acc = acc + jnp.dot(prev_t_ref[q], residual[(i + 1) * rows:(i + 2) * rows], preferred_element_type=single)
            if i > 0:
                acc = acc + jnp.dot(next_t_ref[q], residual[(i - 1) * rows:i * rows], preferred_element_type=single)
            parts.append(acc.astype(bfloat))
        back_wide = jnp.concatenate(parts, axis=0)
        adjoint = adjoint + amp_ref[q] * jnp.dot(back_wide, tall_ref[q], preferred_element_type=single)
    slope = jnp.dot(fetched, slope_ref[...], preferred_element_type=single)
    shift_sum = jnp.sum(adjoint * slope, keepdims=True)
    terms = put(terms, shift_sum, comps)
    terms = terms + jnp.where(lane == EXPO_LANE, expo_ref[0].astype(single), 0.0)
    term_row = terms.astype(bfloat)
    grad = jnp.dot(adjoint.astype(bfloat), interp_t_ref[...], preferred_element_type=single).astype(bfloat)
    place = (
        lax.broadcasted_iota(jnp.int32, (slots, width), 0) == slot_row_ref[...]
    ).astype(bfloat)
    send = jnp.dot(place, grad, preferred_element_type=single).astype(bfloat)
    peers = send_ref.shape[0]
    capacity = send_ref.shape[1] - 1
    for p in range(peers):
        send_ref[p, 0:capacity, :] = send[p * capacity:(p + 1) * capacity]
        send_ref[p, capacity:capacity + 1, :] = term_row


def run_block(amps, expo, slot_index, returned, observed, weight, interp, slope_map, tall, main, prev, nxt, peers):
    width, rows = observed.shape
    slots = returned.shape[0]
    comps = tall.shape[0]
    swap = lambda a: jnp.swapaxes(a, -1, -2)
    vm = pl.BlockSpec(memory_space=pltpu.VMEM)
    sm = pl.BlockSpec(memory_space=pltpu.SMEM)
    return pl.pallas_call(
        block_kernel,
        out_shape=jax.ShapeDtypeStruct((peers, slots // peers + 1, rows), jnp.bfloat16),
        in_specs=[sm, sm] + [vm] * 16,
        out_specs=vm,
        scratch_shapes=[pltpu.VMEM((comps, width, rows), jnp.float32)],
    )(amps, expo, slot_index[:, None], slot_index[None, :], returned, observed, weight, interp,
      swap(interp), slope_map, swap(tall), tall, main, prev, nxt, swap(main), swap(prev), swap(nxt))


def body(
    sky_model,
    observed,
    row_weight,
    foot_owner,
    foot_local,
    row_offset,
    exposure_of,
    amplitude,
    subpixel_shift,
    column_profile,
    row_profile,
):
    tile_count = lax.axis_size("tile")
    seg_count = sky_model.shape[1]
    block_rows = sky_model.shape[2]
    block_count = observed.shape[1]
    width = observed.shape[2]
    capacity = 2 * block_count * width // tile_count
    expo_count = amplitude.shape[1]
    comp_count = amplitude.shape[0]
    tile_blocks = width // block_rows
    requests = block_count * width
    pixels = width * block_rows
    highest = lax.Precision.HIGHEST
    bfloat = jnp.bfloat16
    single = jnp.float32
    request_owner = foot_owner.reshape(requests)
    request_local = foot_local.reshape(requests)
    owner_hits = (
        request_owner.reshape(block_count, width)[:, :, None]
        == jnp.arange(tile_count, dtype=jnp.int32)[None, None, :]
    )
    owner_onehot = owner_hits.astype(bfloat)
    chunk_count = width // block_rows
    owner_chunks = owner_onehot.reshape(block_count, chunk_count, block_rows, tile_count)
    chunk_inner = jnp.einsum(
        "uy,bkyt->bkut", strict_lower(block_rows), owner_chunks, preferred_element_type=single
    )
    chunk_totals = jnp.sum(owner_chunks.astype(single), axis=2)
    chunk_before = jnp.einsum(
        "kl,blt->bkt", strict_lower(chunk_count).astype(single), chunk_totals, precision=highest
    )
    within = (chunk_inner + chunk_before[:, :, None, :]).reshape(block_count, width, tile_count)
    if block_count > 1:
        block_totals = jnp.sum(owner_onehot.astype(single), axis=1)
        before = jnp.dot(strict_lower(block_count).astype(single), block_totals, precision=highest)
        within = within + before[:, None, :]
    rank_table = jnp.where(owner_hits, within, jnp.zeros((), single))
    owner_rank = jnp.sum(rank_table, axis=2).astype(jnp.int32).reshape(requests)
    slot_index = request_owner * capacity + owner_rank
    slot_iota = jnp.arange(tile_count * capacity, dtype=jnp.int32)
    slot_onehot_t = (slot_iota[:, None] == slot_index[None, :]).astype(bfloat)
    request_code = request_local + 1
    request_parts = jnp.stack([request_code // 32, request_code % 32], axis=1).astype(bfloat)
    request_sums = jnp.dot(slot_onehot_t, request_parts, preferred_element_type=single)
    request_ids = (
        request_sums[:, 0].astype(jnp.int32) * 32 + request_sums[:, 1].astype(jnp.int32)
    ).reshape(tile_count, capacity)
    block_offset = row_offset.reshape(block_count)
    block_exposure = exposure_of.reshape(block_count)
    served_ids = lax.all_to_all(request_ids, "tile", split_axis=0, concat_axis=0, tiled=True)
    served_valid = served_ids > 0
    served_where = jnp.maximum(served_ids - 1, 0)
    local_sky = sky_model[0]
    served_flat = served_ids.reshape(tile_count * capacity) - 1
    seg_iota = jnp.arange(seg_count, dtype=jnp.int32)
    serve_onehot = (served_flat[:, None] == seg_iota[None, :]).astype(bfloat)
    picked_rows = jnp.dot(serve_onehot, local_sky, preferred_element_type=single).astype(bfloat)
    served_rows = picked_rows.reshape(tile_count, capacity, block_rows)
    returned = lax.all_to_all(served_rows, "tile", split_axis=0, concat_axis=0, tiled=True)
    expo_onehot = (
        block_exposure[:, None] == jnp.arange(expo_count, dtype=jnp.int32)[None, :]
    ).astype(single)
    block_amp = jnp.dot(expo_onehot, amplitude.T, precision=highest)
    block_frac = jnp.dot(expo_onehot, subpixel_shift, precision=highest)
    block_wide = jnp.einsum("be,eqt->bqt", expo_onehot, column_profile, precision=highest)
    block_tall = jnp.einsum("be,eqt->bqt", expo_onehot, row_profile, precision=highest)
    j_index = jnp.arange(block_rows, dtype=jnp.int32)[None, :, None]
    v_index = jnp.arange(block_rows, dtype=jnp.int32)[None, None, :]
    offsets = block_offset[:, None, None]
    lower_hit = j_index == v_index + offsets
    upper_hit = j_index == v_index + offsets + 1
    zero_b = jnp.zeros((), bfloat)
    weight_low = (1.0 - block_frac).astype(bfloat)[:, None, None]
    weight_high = block_frac.astype(bfloat)[:, None, None]
    interp = jnp.where(lower_hit, weight_low, zero_b) + jnp.where(upper_hit, weight_high, zero_b)
    slope_map = upper_hit.astype(bfloat) - lower_hit.astype(bfloat)
    tall_kernel = band_lookup(block_tall.astype(bfloat), 0, block_rows)
    wide_profile_b = block_wide.astype(bfloat)
    wide_main = band_lookup(wide_profile_b, 0, block_rows)
    wide_prev = band_lookup(wide_profile_b, -block_rows, block_rows)
    wide_next = band_lookup(wide_profile_b, block_rows, block_rows)
    weight_rows = row_weight.reshape(block_count, block_rows)
    observed_blocks = observed[0]
    returned_rows = returned.reshape(tile_count * capacity, block_rows)
    assert block_count == 1
    term_count = comp_count + 1
    send_all = run_block(
        block_amp[0],
        block_exposure,
        slot_index,
        returned_rows,
        observed_blocks[0],
        weight_rows[0][None, :],
        interp[0],
        slope_map[0],
        tall_kernel[0],
        wide_main[0],
        wide_prev[0],
        wide_next[0],
        tile_count,
    )
    received = lax.all_to_all(send_all, "tile", split_axis=0, concat_axis=0, tiled=True)
    segment_rows = received[:, :capacity]
    peer_rows = received[:, capacity, :].astype(single)
    peer_terms = peer_rows[:, :term_count] + peer_rows[:, LOW_LANE : LOW_LANE + term_count]
    peer_onehot = (
        peer_rows[:, EXPO_LANE][:, None] == jnp.arange(expo_count, dtype=single)[None, :]
    ).astype(single)
    partial_params = jnp.dot(peer_terms.T, peer_onehot, precision=highest)
    flat_rows = segment_rows.reshape(tile_count * capacity, block_rows)
    serve_onehot_t = (seg_iota[:, None] == served_flat[None, :]).astype(bfloat)
    grad_local = jnp.dot(serve_onehot_t, flat_rows, preferred_element_type=single)
    grad_params = lax.psum(partial_params, "band")
    return (grad_local[None], grad_params)


def solution(mesh):
    placed = (
        P("band", "tile", None),
        P("band", "tile", None, None),
        P("band", "tile", None),
        P("band", "tile", None, None),
        P("band", "tile", None),
        P("band", "tile"),
        P("band", "tile"),
        P(),
        P(),
        P(),
        P(),
    )
    return jax.shard_map(
        body, mesh=mesh, in_specs=placed, out_specs=(P("band", "tile", None), P()), check_vma=False
    )
```
